512 devices in a mesh: pipe: 8 (over z), space: 64 (over x, y, core).
Axes of the slice: x: 4, y: 8, z: 8, core: 2. Of those that a mesh axis runs over, the one named last changes fastest.
Arguments:
- activations: bfloat16 [8, 2, 96, 256, 512], P('pipe', None, None, 'space'), may hold values from -6 to 6
- cotangent: bfloat16 [8, 2, 96, 256, 512], P('pipe', None, None, 'space'), may hold values from -6 to 6
- kept_modes: int32 [8, 2], P('pipe'), may hold values from 32 to 128, as said below
- weight_in: float32 [8, 2, 2, 96, 96], P('pipe'), may hold values from -0.4375 to 0.4375
- bias_in: float32 [8, 2, 2, 96], P('pipe'), may hold values from -4 to 4
- weight_out: float32 [8, 2, 2, 96, 96], P('pipe'), may hold values from -0.4375 to 0.4375
Outputs:
- grad_input: bfloat16 [8, 2, 96, 256, 512], P('pipe', None, None, 'space')
- grad_weight_in: float32 [8, 2, 2, 96, 96], P('pipe')
- grad_bias_in: float32 [8, 2, 2, 96], P('pipe')
- grad_weight_out: float32 [8, 2, 2, 96, 96], P('pipe')
- grad_bias_out: float32 [8, 2, 2, 96], P('pipe')
The draws below stay inside these ranges and needn't reach their ends.
Inputs may be any that keep to these rules, and one draw needn't show every extreme that they name: `kept_modes`: column 0 is a layer's kept longitude wavenumbers, from 64 to 128, with exactly 128 in some layer; column 1 is the kept latitude wavenumbers of each sign, from 32 to 64, with exactly 64 in some layer.
All inputs are finite; a program needn't handle non-finite values.
Results may differ from the reference program's by a relative error of at most 0.001.
Values may be sent and summed in bfloat16 or wider, within the bound.
No kernel may reach another device: no remote copies, remote signals or barrier semaphores. Data moves between devices by JAX's collectives and lax.ppermute only.
A program may use at most 64 MiB of HBM per device.

```python
import math
import jax
import jax.numpy as jnp
from jax import lax

LAT = 256
LON = 512
KEEP_LON = 128
KEEP_LAT = 64
BLOCK = 96
BLOCKS = 2
LAYERS = 8


def draw_kept_modes(key, part):
    first = jax.random.fold_in(key, 11)
    second = jax.random.fold_in(key, 12)
    third = jax.random.fold_in(key, 13)
    fourth = jax.random.fold_in(key, 14)
    lon_count = jax.random.randint(first, (LAYERS,), KEEP_LON // 2, KEEP_LON + 1)
    lat_count = jax.random.randint(second, (LAYERS,), KEEP_LAT // 2, KEEP_LAT + 1)
    lon_count = lon_count.at[jax.random.randint(third, (), 0, LAYERS)].set(KEEP_LON)
    lat_count = lat_count.at[jax.random.randint(fourth, (), 0, LAYERS)].set(KEEP_LAT)
    return jnp.stack([lon_count, lat_count], axis=1).astype(jnp.int32)


def block_levels(rng, shape, split, least, top_value):
    gain = 1.0
    for axis_at, shards_of in split:
        heights = jax.random.uniform(jax.random.fold_in(jax.random.fold_in(rng, 6), axis_at), (shards_of,), jnp.float32, least / len(split), top_value / len(split))
        gain = gain * jnp.repeat(jnp.exp(heights), shape[axis_at] // shards_of).reshape((-1,) + (1,) * (len(shape) - 1 - axis_at))
    return gain


def gaussian(stream_key, dims, scale, reach, split=(), held_as=jnp.bfloat16):
    factor_of = block_levels(stream_key, dims, split, -0.22, 0.18) if split else 1.0
    values = jax.random.normal(stream_key, dims, jnp.float32) * scale * factor_of
    return jnp.minimum(jnp.maximum(values, -reach), reach).astype(held_as)


def setup_inputs(seed: int = 0) -> dict:
    splits = jax.random.split(jax.random.key(seed), 7)
    return {
        "activations": gaussian(splits[0], (LAYERS, BLOCKS, BLOCK, LAT, LON), 1.0, 6.0, ((0, 8), (3, 64))),
        "cotangent": gaussian(splits[1], (LAYERS, BLOCKS, BLOCK, LAT, LON), 1.0, 6.0, ((0, 8), (3, 64))),
        "kept_modes": draw_kept_modes(jax.random.fold_in(splits[6], 71), 0),
        "weight_in": gaussian(splits[3], (LAYERS, 2, BLOCKS, BLOCK, BLOCK), (2 * BLOCK) ** -0.5, 0.4375, ((0, 8),), jnp.float32),
        "bias_in": gaussian(splits[4], (LAYERS, 2, BLOCKS, BLOCK), 1.0, 4.0, ((0, 8),), jnp.float32),
        "weight_out": gaussian(splits[5], (LAYERS, 2, BLOCKS, BLOCK, BLOCK), (2 * BLOCK) ** -0.5, 0.4375, ((0, 8),), jnp.float32),
    }


HIGHEST = lax.Precision.HIGHEST

def lon_tables(length, count):
    column = jnp.arange(length, dtype=jnp.int32)
    number = jnp.arange(count, dtype=jnp.int32)
    phase = column[:, None] * number[None, :] % length
    angle = phase.astype(jnp.float32) * (2.0 * math.pi / length)
    factor = 1.0 / math.sqrt(length)
    return (jnp.cos(angle) * factor, jnp.sin(angle) * factor)

def lat_tables(length, half):
    signed = jnp.arange(2 * half, dtype=jnp.int32) - half
    row_index = jnp.arange(length, dtype=jnp.int32)
    phase = signed[:, None] * row_index[None, :] % length
    angle = phase.astype(jnp.float32) * (2.0 * math.pi / length)
    factor = 1.0 / math.sqrt(length)
    return (jnp.cos(angle) * factor, jnp.sin(angle) * factor)

def lon_forward(field, cos_table, sin_table):
    values = field.astype(jnp.float32)
    real_part = jnp.einsum('ibln,nk->iblk', values, cos_table, precision=HIGHEST)
    imag_part = -jnp.einsum('ibln,nk->iblk', values, sin_table, precision=HIGHEST)
    return jnp.stack([real_part, imag_part])

def lat_forward(spectrum, cos_table, sin_table):

    def apply(table, values):
        return jnp.einsum('fl,ibln->ibfn', table, values, precision=HIGHEST)
    real_part = apply(cos_table, spectrum[0]) + apply(sin_table, spectrum[1])
    imag_part = apply(cos_table, spectrum[1]) - apply(sin_table, spectrum[0])
    return jnp.stack([real_part, imag_part])

def lat_inverse(spectrum, cos_table, sin_table):

    def apply(table, values):
        return jnp.einsum('fl,ibfn->ibln', table, values, precision=HIGHEST)
    real_part = apply(cos_table, spectrum[0]) - apply(sin_table, spectrum[1])
    imag_part = apply(cos_table, spectrum[1]) + apply(sin_table, spectrum[0])
    return jnp.stack([real_part, imag_part])

def lon_inverse(spectrum, cos_table, sin_table):
    first = jnp.einsum('iblk,nk->ibln', spectrum[0], cos_table, precision=HIGHEST)
    second = jnp.einsum('iblk,nk->ibln', spectrum[1], sin_table, precision=HIGHEST)
    return first - second

def mode_weight(wavenumber, keep_lon, keep_lat, half):
    signed = jnp.arange(2 * half, dtype=jnp.int32) - half
    lat_kept = (signed >= -keep_lat) & (signed < keep_lat)
    lon_kept = wavenumber < keep_lon
    factor = jnp.where(wavenumber == 0, 1.0, 2.0).astype(jnp.float32)
    return (lat_kept[:, None] & lon_kept[None, :]).astype(jnp.float32) * factor[None, :]

def block_product(weights, values):
    return jnp.einsum('kij,kjm->kim', weights, values, precision=HIGHEST)

def complex_apply(weights, values):
    real_part = block_product(weights[0], values[0]) - block_product(weights[1], values[1])
    imag_part = block_product(weights[1], values[0]) + block_product(weights[0], values[1])
    return jnp.stack([real_part, imag_part])

def complex_adjoint(weights, values):
    real_t = jnp.swapaxes(weights[0], 1, 2)
    imag_t = jnp.swapaxes(weights[1], 1, 2)
    real_part = block_product(real_t, values[0]) + block_product(imag_t, values[1])
    imag_part = block_product(real_t, values[1]) - block_product(imag_t, values[0])
    return jnp.stack([real_part, imag_part])

def complex_outer(left, right):

    def outer(first, second):
        return jnp.einsum('kim,kjm->kij', first, second, precision=HIGHEST)
    real_part = outer(left[0], right[0]) + outer(left[1], right[1])
    imag_part = outer(left[1], right[0]) - outer(left[0], right[1])
    return jnp.stack([real_part, imag_part])

def gelu_pair(values):
    inner = 0.7978845608 * (values + 0.044715 * values * values * values)
    tangent = jnp.tanh(inner)
    output = 0.5 * values * (1.0 + tangent)
    slope = 0.5 * (1.0 + tangent) + 0.5 * values * (1.0 - tangent * tangent) * 0.7978845608 * (1.0 + 3.0 * 0.044715 * values * values)
    return (output, slope)

def backprop(spectrum, grad_spec, weight_in, bias_in, weight_out):
    before = complex_apply(weight_in, spectrum) + bias_in[..., None]
    hidden, slope = gelu_pair(before)
    grad_hidden = complex_adjoint(weight_out, grad_spec)
    grad_before = grad_hidden * slope
    grad_modes = complex_adjoint(weight_in, grad_before)
    grad_w_out = complex_outer(grad_spec, hidden)
    grad_w_in = complex_outer(grad_before, spectrum)
    return (grad_modes, grad_w_in, lax.optimization_barrier(jnp.sum(grad_before, axis=-1)), grad_w_out, lax.optimization_barrier(jnp.sum(grad_spec, axis=-1)))

def reference(activations, cotangent, kept_modes, weight_in, bias_in, weight_out):
    layer_count = activations.shape[0]
    nblocks = activations.shape[1]
    width = activations.shape[2]
    lon_cos, lon_sin = lon_tables(LON, KEEP_LON)
    lat_cos, lat_sin = lat_tables(LAT, KEEP_LAT)
    factor = 1.0 / math.sqrt(2 * KEEP_LAT * KEEP_LON)
    wavenumber = jnp.arange(KEEP_LON, dtype=jnp.int32)
    results = [[], [], [], [], []]
    for layer in range(layer_count):
        field = activations[layer]
        upstream = cotangent[min(layer + 1, layer_count - 1)]
        weight = mode_weight(wavenumber, kept_modes[layer, 0], kept_modes[layer, 1], KEEP_LAT)
        spectrum = lat_forward(lon_forward(field, lon_cos, lon_sin), lat_cos, lat_sin)
        grad_spec = lat_forward(lon_forward(upstream, lon_cos, lon_sin), lat_cos, lat_sin) * weight
        spectrum = spectrum.reshape(2, nblocks, width, -1)
        grad_spec = grad_spec.reshape(2, nblocks, width, -1)
        grad_modes, grad_w_in, grad_b_in, grad_w_out, grad_b_out = backprop(spectrum, grad_spec, weight_in[layer], bias_in[layer], weight_out[layer])
        grad_modes = grad_modes.reshape(2, nblocks, width, 2 * KEEP_LAT, KEEP_LON)
        back = lat_inverse(grad_modes, lat_cos, lat_sin)
        grad_field = (upstream.astype(jnp.float32) + lon_inverse(back, lon_cos, lon_sin)).astype(jnp.bfloat16)
        results[0].append(grad_field)
        results[1].append(grad_w_in * factor)
        results[2].append(grad_b_in * factor)
        results[3].append(grad_w_out * factor)
        results[4].append(grad_b_out * factor)
    return (jnp.stack(results[0]), jnp.stack(results[1]), jnp.stack(results[2]), jnp.stack(results[3]), jnp.stack(results[4]))
```

```python
import math

import jax
import jax.numpy as jnp
from jax import lax
from jax.sharding import PartitionSpec as P

LAT = 256
LON = 512
KEEP_LON = 128
KEEP_LAT = 64


HIGHEST = lax.Precision.HIGHEST


def from_behind(block, axis, distance):
    devices = range(lax.axis_size(axis))
    route = [(i - distance, i) for i in devices if i - distance in devices]
    return lax.ppermute(block, axis, route)


def lon_tables(length, count):
    column = jnp.arange(length, dtype=jnp.int32)
    number = jnp.arange(count, dtype=jnp.int32)
    phase = column[:, None] * number[None, :] % length
    angle = phase.astype(jnp.float32) * (2.0 * math.pi / length)
    factor = 1.0 / math.sqrt(length)
    return (jnp.cos(angle) * factor, jnp.sin(angle) * factor)


def lat_tables(length, half):
    signed = jnp.arange(2 * half, dtype=jnp.int32) - half
    row_index = jnp.arange(length, dtype=jnp.int32)
    phase = signed[:, None] * row_index[None, :] % length
    angle = phase.astype(jnp.float32) * (2.0 * math.pi / length)
    factor = 1.0 / math.sqrt(length)
    return (jnp.cos(angle) * factor, jnp.sin(angle) * factor)


def lon_forward_table(cos_table, sin_table, ndev):
    share = cos_table.shape[1] // ndev
    cos_g = cos_table.reshape(-1, ndev, 1, share)
    sin_g = -sin_table.reshape(-1, ndev, 1, share)
    return jnp.concatenate([cos_g, sin_g], axis=2).reshape(cos_table.shape[0], -1)


def lon_forward(field, table):
    values = field.astype(jnp.float32)
    return jnp.einsum("ibln,nc->iblc", values, table, precision=HIGHEST)


def lat_forward(spectrum, cos_table, sin_table):
    top = jnp.stack([cos_table, sin_table], axis=1)
    bottom = jnp.stack([-sin_table, cos_table], axis=1)
    table = jnp.stack([top, bottom])
    return jnp.einsum("ofpl,iblpj->oibfj", table, spectrum, precision=HIGHEST)


def lat_inverse(spectrum, cos_table, sin_table):
    top = jnp.stack([cos_table, -sin_table])
    bottom = jnp.stack([sin_table, cos_table])
    table = jnp.stack([top, bottom])
    return jnp.einsum("opfl,pibfj->oiblj", table, spectrum, precision=HIGHEST)


def lon_inverse(spectrum, cos_table, sin_table):
    table = jnp.stack([cos_table, -sin_table])
    return jnp.einsum("piblk,pnk->ibln", spectrum, table, precision=HIGHEST)


def mode_mask(signed, wavenumber, keep_lon, keep_lat):
    lat_kept = (signed >= -keep_lat) & (signed < keep_lat)
    lon_kept = wavenumber < keep_lon
    factor = jnp.where(wavenumber == 0, 1.0, 2.0).astype(jnp.float32)
    return (lat_kept[:, None] & lon_kept[None, :]).astype(jnp.float32) * factor[None, :]


def block_product(weights, values):
    return jnp.einsum("kij,kjm->kim", weights, values, precision=HIGHEST)


def complex_apply(weights, values):
    real_part = block_product(weights[0], values[0]) - block_product(weights[1], values[1])
    imag_part = block_product(weights[1], values[0]) + block_product(weights[0], values[1])
    return jnp.stack([real_part, imag_part])


def complex_adjoint(weights, values):
    real_t = jnp.swapaxes(weights[0], 1, 2)
    imag_t = jnp.swapaxes(weights[1], 1, 2)
    real_part = block_product(real_t, values[0]) + block_product(imag_t, values[1])
    imag_part = block_product(real_t, values[1]) - block_product(imag_t, values[0])
    return jnp.stack([real_part, imag_part])


def complex_outer(left, right):

    def outer(first, second):
        return jnp.einsum("kim,kjm->kij", first, second, precision=HIGHEST)

    real_part = outer(left[0], right[0]) + outer(left[1], right[1])
    imag_part = outer(left[1], right[0]) - outer(left[0], right[1])
    return jnp.stack([real_part, imag_part])


def gelu_pair(values):
    inner = 0.7978845608 * (values + 0.044715 * values * values * values)
    tangent = jnp.tanh(inner)
    output = 0.5 * values * (1.0 + tangent)
    slope = 0.5 * (1.0 + tangent) + 0.5 * values * (1.0 - tangent * tangent) * 0.7978845608 * (
        1.0 + 3.0 * 0.044715 * values * values
    )
    return (output, slope)


def backprop(spectrum, grad_spec, weight_in, bias_in, weight_out):
    before = complex_apply(weight_in, spectrum) + bias_in[..., None]
    hidden, slope = gelu_pair(before)
    grad_hidden = complex_adjoint(weight_out, grad_spec)
    grad_before = grad_hidden * slope
    grad_modes = complex_adjoint(weight_in, grad_before)
    grad_w_out = complex_outer(grad_spec, hidden)
    grad_w_in = complex_outer(grad_before, spectrum)
    return (
        grad_modes,
        grad_w_in,
        jnp.sum(grad_before, axis=-1),
        grad_w_out,
        jnp.sum(grad_spec, axis=-1),
    )


def to_columns(spectrum, ndev):
    moved = lax.all_to_all(spectrum, "space", split_axis=3, concat_axis=2, tiled=True)
    nblocks, width, rows, _ = moved.shape
    return moved.reshape(nblocks, width, rows, 2, -1)


def shards(activations, cotangent, kept_modes, weight_in, bias_in, weight_out):
    field = activations[0]
    own_grad = cotangent[0]
    nblocks = field.shape[0]
    width = field.shape[1]
    ndev = lax.axis_size("space")
    received = from_behind(own_grad, "pipe", -1)
    section_index = lax.axis_index("pipe")
    last_section = lax.axis_size("pipe") - 1
    upstream = jnp.where(section_index == last_section, own_grad, received)
    lon_cos, lon_sin = lon_tables(LON, KEEP_LON)
    lat_cos, lat_sin = lat_tables(LAT, KEEP_LAT)
    table = lon_forward_table(lon_cos, lon_sin, ndev)
    col_field = to_columns(lon_forward(field, table), ndev)
    col_grad = to_columns(lon_forward(upstream, table), ndev)
    spectrum = lat_forward(col_field, lat_cos, lat_sin)
    grad_spec = lat_forward(col_grad, lat_cos, lat_sin)
    share = KEEP_LON // ndev
    signed = jnp.arange(2 * KEEP_LAT, dtype=jnp.int32) - KEEP_LAT
    wavenumber = lax.axis_index("space") * share + jnp.arange(share, dtype=jnp.int32)
    weight = mode_mask(signed, wavenumber, kept_modes[0, 0], kept_modes[0, 1])
    grad_spec = grad_spec * weight
    spectrum = spectrum.reshape(2, nblocks, width, -1)
    grad_spec = grad_spec.reshape(2, nblocks, width, -1)
    grad_modes, grad_w_in, grad_b_in, grad_w_out, grad_b_out = backprop(
        spectrum, grad_spec, weight_in[0], bias_in[0], weight_out[0]
    )
    grad_modes = grad_modes.reshape(2, nblocks, width, 2 * KEEP_LAT, share)
    lat_back = lat_inverse(grad_modes, lat_cos, lat_sin)
    rows_back = lax.all_to_all(lat_back, "space", split_axis=3, concat_axis=4, tiled=True)
    inverse = lon_inverse(rows_back, lon_cos, lon_sin)
    parts = (grad_w_in, grad_b_in, grad_w_out, grad_b_out)
    flat = lax.psum(jnp.concatenate([p.reshape(-1) for p in parts]), "space")
    factor = 1.0 / math.sqrt(2 * KEEP_LAT * KEEP_LON)
    flat = flat * factor
    sums = []
    start = 0
    for p in parts:
        sums.append(flat[start:start + p.size].reshape(p.shape)[None])
        start += p.size
    grad_field = (upstream.astype(jnp.float32) + inverse).astype(jnp.bfloat16)
    return (grad_field[None], *sums)


def solution(mesh):
    return jax.shard_map(
        shards,
        mesh=mesh,
        in_specs=(
            P("pipe", None, None, "space", None),
            P("pipe", None, None, "space", None),
            P("pipe", None),
            P("pipe", None, None, None, None),
            P("pipe", None, None, None),
            P("pipe", None, None, None, None),
        ),
        out_specs=(
            P("pipe", None, None, "space", None),
            P("pipe", None, None, None, None),
            P("pipe", None, None, None),
            P("pipe", None, None, None, None),
            P("pipe", None, None, None),
        ),
        check_vma=False,
    )
```

```python
import math

import jax
import jax.numpy as jnp
from jax import lax
from jax.sharding import PartitionSpec as P

LAT = 256
LON = 512
KEEP_LON = 128
KEEP_LAT = 64


HIGHEST = lax.Precision.HIGHEST


def from_behind(block, axis, distance):
    devices = range(lax.axis_size(axis))
    route = [(i - distance, i) for i in devices if i - distance in devices]
    return lax.ppermute(block, axis, route)


def lon_tables(length, count):
    column = jnp.arange(length, dtype=jnp.int32)
    number = jnp.arange(count, dtype=jnp.int32)
    phase = column[:, None] * number[None, :] % length
    angle = phase.astype(jnp.float32) * (2.0 * math.pi / length)
    factor = 1.0 / math.sqrt(length)
    return (jnp.cos(angle) * factor, jnp.sin(angle) * factor)


def lat_tables(length, half):
    signed = jnp.arange(2 * half, dtype=jnp.int32) - half
    row_index = jnp.arange(length, dtype=jnp.int32)
    phase = signed[:, None] * row_index[None, :] % length
    angle = phase.astype(jnp.float32) * (2.0 * math.pi / length)
    factor = 1.0 / math.sqrt(length)
    return (jnp.cos(angle) * factor, jnp.sin(angle) * factor)


def lon_forward_table(cos_table, sin_table, ndev):
    share = cos_table.shape[1] // ndev
    cos_g = cos_table.reshape(-1, ndev, 1, share)
    sin_g = -sin_table.reshape(-1, ndev, 1, share)
    return jnp.concatenate([cos_g, sin_g], axis=2).reshape(cos_table.shape[0], -1)


def lon_forward(field, table):
    values = field.astype(jnp.float32)
    return jnp.einsum("ibln,nc->iblc", values, table, precision=HIGHEST)


def lat_forward(spectrum, cos_table, sin_table):
    top = jnp.stack([cos_table, sin_table], axis=1)
    bottom = jnp.stack([-sin_table, cos_table], axis=1)
    table = jnp.stack([top, bottom])
    return jnp.einsum("ofpl,iblpj->oibfj", table, spectrum, precision=HIGHEST)


def lat_inverse(spectrum, cos_table, sin_table):
    top = jnp.stack([cos_table, -sin_table])
    bottom = jnp.stack([sin_table, cos_table])
    table = jnp.stack([top, bottom])
    return jnp.einsum("opfl,pibfj->oiblj", table, spectrum, precision=HIGHEST)


def lon_inverse(spectrum, cos_table, sin_table):
    table = jnp.stack([cos_table, -sin_table])
    return jnp.einsum("piblk,pnk->ibln", spectrum, table, precision=HIGHEST)


def mode_mask(signed, wavenumber, keep_lon, keep_lat):
    lat_kept = (signed >= -keep_lat) & (signed < keep_lat)
    lon_kept = wavenumber < keep_lon
    factor = jnp.where(wavenumber == 0, 1.0, 2.0).astype(jnp.float32)
    return (lat_kept[:, None] & lon_kept[None, :]).astype(jnp.float32) * factor[None, :]


def block_product(weights, values):
    return jnp.einsum("kij,kjm->kim", weights, values, precision=HIGHEST)


def complex_apply(weights, values):
    real_part = block_product(weights[0], values[0]) - block_product(weights[1], values[1])
    imag_part = block_product(weights[1], values[0]) + block_product(weights[0], values[1])
    return jnp.stack([real_part, imag_part])


def complex_adjoint(weights, values):
    real_t = jnp.swapaxes(weights[0], 1, 2)
    imag_t = jnp.swapaxes(weights[1], 1, 2)
    real_part = block_product(real_t, values[0]) + block_product(imag_t, values[1])
    imag_part = block_product(real_t, values[1]) - block_product(imag_t, values[0])
    return jnp.stack([real_part, imag_part])


def complex_outer(left, right):

    def outer(first, second):
        return jnp.einsum("kim,kjm->kij", first, second, precision=HIGHEST)

    real_part = outer(left[0], right[0]) + outer(left[1], right[1])
    imag_part = outer(left[1], right[0]) - outer(left[0], right[1])
    return jnp.stack([real_part, imag_part])


def gelu_pair(values):
    inner = 0.7978845608 * (values + 0.044715 * values * values * values)
    tangent = jnp.tanh(inner)
    output = 0.5 * values * (1.0 + tangent)
    slope = 0.5 * (1.0 + tangent) + 0.5 * values * (1.0 - tangent * tangent) * 0.7978845608 * (
        1.0 + 3.0 * 0.044715 * values * values
    )
    return (output, slope)


def backprop(spectrum, grad_spec, weight_in, bias_in, weight_out):
    before = complex_apply(weight_in, spectrum) + bias_in[..., None]
    hidden, slope = gelu_pair(before)
    grad_hidden = complex_adjoint(weight_out, grad_spec)
    grad_before = grad_hidden * slope
    grad_modes = complex_adjoint(weight_in, grad_before)
    grad_w_out = complex_outer(grad_spec, hidden)
    grad_w_in = complex_outer(grad_before, spectrum)
    return (
        grad_modes,
        grad_w_in,
        jnp.sum(grad_before, axis=-1),
        grad_w_out,
        jnp.sum(grad_spec, axis=-1),
    )


def to_columns(spectrum, ndev):
    moved = lax.all_to_all(spectrum, "space", split_axis=3, concat_axis=2, tiled=True)
    nblocks, width, rows, _ = moved.shape
    return moved.reshape(nblocks, width, rows, 2, -1)


def sum_over(flat, axis):
    n = lax.axis_size(axis)
    pad = (-flat.shape[0]) % n
    pieces = jnp.pad(flat, (0, pad)).reshape(n, -1)
    got = lax.all_to_all(pieces, axis, split_axis=0, concat_axis=0, tiled=True)
    mine = jnp.sum(got, axis=0)
    spread = jnp.broadcast_to(mine[None], pieces.shape)
    full = lax.all_to_all(spread, axis, split_axis=0, concat_axis=0, tiled=True)
    return full.reshape(-1)[: flat.shape[0]]


def shards(activations, cotangent, kept_modes, weight_in, bias_in, weight_out):
    field = activations[0]
    own_grad = cotangent[0]
    nblocks = field.shape[0]
    width = field.shape[1]
    ndev = lax.axis_size("space")
    received = from_behind(own_grad, "pipe", -1)
    section_index = lax.axis_index("pipe")
    last_section = lax.axis_size("pipe") - 1
    upstream = jnp.where(section_index == last_section, own_grad, received)
    lon_cos, lon_sin = lon_tables(LON, KEEP_LON)
    lat_cos, lat_sin = lat_tables(LAT, KEEP_LAT)
    table = lon_forward_table(lon_cos, lon_sin, ndev)
    col_field = to_columns(lon_forward(field, table), ndev)
    col_grad = to_columns(lon_forward(upstream, table), ndev)
    spectrum = lat_forward(col_field, lat_cos, lat_sin)
    grad_spec = lat_forward(col_grad, lat_cos, lat_sin)
    share = KEEP_LON // ndev
    signed = jnp.arange(2 * KEEP_LAT, dtype=jnp.int32) - KEEP_LAT
    wavenumber = lax.axis_index("space") * share + jnp.arange(share, dtype=jnp.int32)
    weight = mode_mask(signed, wavenumber, kept_modes[0, 0], kept_modes[0, 1])
    grad_spec = grad_spec * weight
    spectrum = spectrum.reshape(2, nblocks, width, -1)
    grad_spec = grad_spec.reshape(2, nblocks, width, -1)
    grad_modes, grad_w_in, grad_b_in, grad_w_out, grad_b_out = backprop(
        spectrum, grad_spec, weight_in[0], bias_in[0], weight_out[0]
    )
    grad_modes = grad_modes.reshape(2, nblocks, width, 2 * KEEP_LAT, share)
    lat_back = lat_inverse(grad_modes, lat_cos, lat_sin)
    rows_back = lax.all_to_all(lat_back, "space", split_axis=3, concat_axis=4, tiled=True)
    inverse = lon_inverse(rows_back, lon_cos, lon_sin)
    parts = (grad_w_in, grad_b_in, grad_w_out, grad_b_out)
    flat = sum_over(jnp.concatenate([p.reshape(-1) for p in parts]), "space")
    factor = 1.0 / math.sqrt(2 * KEEP_LAT * KEEP_LON)
    flat = flat * factor
    sums = []
    start = 0
    for p in parts:
        sums.append(flat[start:start + p.size].reshape(p.shape)[None])
        start += p.size
    grad_field = (upstream.astype(jnp.float32) + inverse).astype(jnp.bfloat16)
    return (grad_field[None], *sums)


def solution(mesh):
    return jax.shard_map(
        shards,
        mesh=mesh,
        in_specs=(
            P("pipe", None, None, "space", None),
            P("pipe", None, None, "space", None),
            P("pipe", None),
            P("pipe", None, None, None, None),
            P("pipe", None, None, None),
            P("pipe", None, None, None, None),
        ),
        out_specs=(
            P("pipe", None, None, "space", None),
            P("pipe", None, None, None, None),
            P("pipe", None, None, None),
            P("pipe", None, None, None, None),
            P("pipe", None, None, None),
        ),
        check_vma=False,
    )
```

```python
import math

import jax
import jax.numpy as jnp
from jax import lax
from jax.sharding import PartitionSpec as P

LAT = 256
LON = 512
KEEP_LON = 128
KEEP_LAT = 64


HIGHEST = lax.Precision.HIGH


def from_behind(block, axis, distance):
    devices = range(lax.axis_size(axis))
    route = [(i - distance, i) for i in devices if i - distance in devices]
    return lax.ppermute(block, axis, route)


def lon_tables(length, count):
    column = jnp.arange(length, dtype=jnp.int32)
    number = jnp.arange(count, dtype=jnp.int32)
    phase = column[:, None] * number[None, :] % length
    angle = phase.astype(jnp.float32) * (2.0 * math.pi / length)
    factor = 1.0 / math.sqrt(length)
    return (jnp.cos(angle) * factor, jnp.sin(angle) * factor)


def lat_tables(length, half):
    signed = jnp.arange(2 * half, dtype=jnp.int32) - half
    row_index = jnp.arange(length, dtype=jnp.int32)
    phase = signed[:, None] * row_index[None, :] % length
    angle = phase.astype(jnp.float32) * (2.0 * math.pi / length)
    factor = 1.0 / math.sqrt(length)
    return (jnp.cos(angle) * factor, jnp.sin(angle) * factor)


def lon_forward_table(cos_table, sin_table, ndev):
    share = cos_table.shape[1] // ndev
    cos_g = cos_table.reshape(-1, ndev, 1, share)
    sin_g = -sin_table.reshape(-1, ndev, 1, share)
    return jnp.concatenate([cos_g, sin_g], axis=2).reshape(cos_table.shape[0], -1)


def lon_forward(field, table):
    values = field.astype(jnp.float32)
    return jnp.einsum("ibln,nc->iblc", values, table, precision=HIGHEST)


def lat_forward(spectrum, cos_table, sin_table):
    top = jnp.stack([cos_table, sin_table], axis=1)
    bottom = jnp.stack([-sin_table, cos_table], axis=1)
    table = jnp.stack([top, bottom])
    return jnp.einsum("ofpl,iblpj->oibfj", table, spectrum, precision=HIGHEST)


def lat_inverse(spectrum, cos_table, sin_table):
    top = jnp.stack([cos_table, -sin_table])
    bottom = jnp.stack([sin_table, cos_table])
    table = jnp.stack([top, bottom])
    return jnp.einsum("opfl,pibfj->oiblj", table, spectrum, precision=HIGHEST)


def lon_inverse(spectrum, cos_table, sin_table):
    table = jnp.stack([cos_table, -sin_table])
    return jnp.einsum("piblk,pnk->ibln", spectrum, table, precision=HIGHEST)


def mode_mask(signed, wavenumber, keep_lon, keep_lat):
    lat_kept = (signed >= -keep_lat) & (signed < keep_lat)
    lon_kept = wavenumber < keep_lon
    factor = jnp.where(wavenumber == 0, 1.0, 2.0).astype(jnp.float32)
    return (lat_kept[:, None] & lon_kept[None, :]).astype(jnp.float32) * factor[None, :]


def block_product(weights, values):
    return jnp.einsum("kij,kjm->kim", weights, values, precision=HIGHEST)


def complex_apply(weights, values):
    real_part = block_product(weights[0], values[0]) - block_product(weights[1], values[1])
    imag_part = block_product(weights[1], values[0]) + block_product(weights[0], values[1])
    return jnp.stack([real_part, imag_part])


def complex_adjoint(weights, values):
    real_t = jnp.swapaxes(weights[0], 1, 2)
    imag_t = jnp.swapaxes(weights[1], 1, 2)
    real_part = block_product(real_t, values[0]) + block_product(imag_t, values[1])
    imag_part = block_product(real_t, values[1]) - block_product(imag_t, values[0])
    return jnp.stack([real_part, imag_part])


def complex_outer(left, right):

    def outer(first, second):
        return jnp.einsum("kim,kjm->kij", first, second, precision=HIGHEST)

    real_part = outer(left[0], right[0]) + outer(left[1], right[1])
    imag_part = outer(left[1], right[0]) - outer(left[0], right[1])
    return jnp.stack([real_part, imag_part])


def gelu_pair(values):
    inner = 0.7978845608 * (values + 0.044715 * values * values * values)
    tangent = jnp.tanh(inner)
    output = 0.5 * values * (1.0 + tangent)
    slope = 0.5 * (1.0 + tangent) + 0.5 * values * (1.0 - tangent * tangent) * 0.7978845608 * (
        1.0 + 3.0 * 0.044715 * values * values
    )
    return (output, slope)


def backprop(spectrum, grad_spec, weight_in, bias_in, weight_out):
    before = complex_apply(weight_in, spectrum) + bias_in[..., None]
    hidden, slope = gelu_pair(before)
    grad_hidden = complex_adjoint(weight_out, grad_spec)
    grad_before = grad_hidden * slope
    grad_modes = complex_adjoint(weight_in, grad_before)
    grad_w_out = complex_outer(grad_spec, hidden)
    grad_w_in = complex_outer(grad_before, spectrum)
    return (
        grad_modes,
        grad_w_in,
        jnp.sum(grad_before, axis=-1),
        grad_w_out,
        jnp.sum(grad_spec, axis=-1),
    )


def to_columns(spectrum, ndev):
    moved = lax.all_to_all(spectrum, "space", split_axis=3, concat_axis=2, tiled=True)
    nblocks, width, rows, _ = moved.shape
    return moved.reshape(nblocks, width, rows, 2, -1)


def sum_over(flat, axis):
    n = lax.axis_size(axis)
    pad = (-flat.shape[0]) % n
    pieces = jnp.pad(flat, (0, pad)).reshape(n, -1)
    got = lax.all_to_all(pieces, axis, split_axis=0, concat_axis=0, tiled=True)
    mine = jnp.sum(got, axis=0)
    spread = jnp.broadcast_to(mine[None], pieces.shape)
    full = lax.all_to_all(spread, axis, split_axis=0, concat_axis=0, tiled=True)
    return full.reshape(-1)[: flat.shape[0]]


def shards(activations, cotangent, kept_modes, weight_in, bias_in, weight_out):
    field = activations[0]
    own_grad = cotangent[0]
    nblocks = field.shape[0]
    width = field.shape[1]
    ndev = lax.axis_size("space")
    received = from_behind(own_grad, "pipe", -1)
    section_index = lax.axis_index("pipe")
    last_section = lax.axis_size("pipe") - 1
    lon_cos, lon_sin = lon_tables(LON, KEEP_LON)
    lat_cos, lat_sin = lat_tables(LAT, KEEP_LAT)
    table = lon_forward_table(lon_cos, lon_sin, ndev)
    col_field = to_columns(lon_forward(field, table), ndev)
    spectrum = lat_forward(col_field, lat_cos, lat_sin)
    spectrum, received = lax.optimization_barrier((spectrum, received))
    upstream = jnp.where(section_index == last_section, own_grad, received)
    col_grad = to_columns(lon_forward(upstream, table), ndev)
    grad_spec = lat_forward(col_grad, lat_cos, lat_sin)
    share = KEEP_LON // ndev
    signed = jnp.arange(2 * KEEP_LAT, dtype=jnp.int32) - KEEP_LAT
    wavenumber = lax.axis_index("space") * share + jnp.arange(share, dtype=jnp.int32)
    weight = mode_mask(signed, wavenumber, kept_modes[0, 0], kept_modes[0, 1])
    grad_spec = grad_spec * weight
    spectrum = spectrum.reshape(2, nblocks, width, -1)
    grad_spec = grad_spec.reshape(2, nblocks, width, -1)
    grad_modes, grad_w_in, grad_b_in, grad_w_out, grad_b_out = backprop(
        spectrum, grad_spec, weight_in[0], bias_in[0], weight_out[0]
    )
    grad_modes = grad_modes.reshape(2, nblocks, width, 2 * KEEP_LAT, share)
    lat_back = lat_inverse(grad_modes, lat_cos, lat_sin)
    parts = (grad_w_in, grad_b_in, grad_w_out, grad_b_out)
    flat = jnp.concatenate([p.reshape(-1) for p in parts])
    pad = (-flat.shape[0]) % ndev
    pieces = jnp.pad(flat, (0, pad)).reshape(ndev, -1)
    rows = LAT // ndev
    back = lat_back.reshape(2, nblocks, width, ndev, rows, share)
    back = jnp.moveaxis(back, 3, 0).reshape(ndev, -1)
    moved = lax.all_to_all(
        jnp.concatenate([back, pieces], axis=1), "space", split_axis=0, concat_axis=0, tiled=True
    )
    rows_back = moved[:, : back.shape[1]].reshape(ndev, 2, nblocks, width, rows, share)
    rows_back = jnp.moveaxis(rows_back, 0, 4).reshape(2, nblocks, width, rows, ndev * share)
    mine = jnp.sum(moved[:, back.shape[1]:], axis=0)
    spread = jnp.broadcast_to(mine[None], pieces.shape)
    flat = lax.all_to_all(spread, "space", split_axis=0, concat_axis=0, tiled=True)
    flat = flat.reshape(-1)[: flat.size - pad]
    inverse = lon_inverse(rows_back, lon_cos, lon_sin)
    factor = 1.0 / math.sqrt(2 * KEEP_LAT * KEEP_LON)
    flat = flat * factor
    sums = []
    start = 0
    for p in parts:
        sums.append(flat[start:start + p.size].reshape(p.shape)[None])
        start += p.size
    grad_field = (upstream.astype(jnp.float32) + inverse).astype(jnp.bfloat16)
    return (grad_field[None], *sums)


def solution(mesh):
    return jax.shard_map(
        shards,
        mesh=mesh,
        in_specs=(
            P("pipe", None, None, "space", None),
            P("pipe", None, None, "space", None),
            P("pipe", None),
            P("pipe", None, None, None, None),
            P("pipe", None, None, None),
            P("pipe", None, None, None, None),
        ),
        out_specs=(
            P("pipe", None, None, "space", None),
            P("pipe", None, None, None, None),
            P("pipe", None, None, None),
            P("pipe", None, None, None, None),
            P("pipe", None, None, None),
        ),
        check_vma=False,
    )
```

```python
import math

import jax
import jax.numpy as jnp
from jax import lax
from jax.sharding import Mesh, PartitionSpec as P

LAT = 256
LON = 512
KEEP_LON = 128
KEEP_LAT = 64


HIGHEST = lax.Precision.HIGH


def from_behind(block, axis, distance):
    devices = range(lax.axis_size(axis))
    route = [(i - distance, i) for i in devices if i - distance in devices]
    return lax.ppermute(block, axis, route)


def lon_tables(length, count):
    column = jnp.arange(length, dtype=jnp.int32)
    number = jnp.arange(count, dtype=jnp.int32)
    phase = column[:, None] * number[None, :] % length
    angle = phase.astype(jnp.float32) * (2.0 * math.pi / length)
    factor = 1.0 / math.sqrt(length)
    return (jnp.cos(angle) * factor, jnp.sin(angle) * factor)


def lat_tables(length, half):
    signed = jnp.arange(2 * half, dtype=jnp.int32) - half
    row_index = jnp.arange(length, dtype=jnp.int32)
    phase = signed[:, None] * row_index[None, :] % length
    angle = phase.astype(jnp.float32) * (2.0 * math.pi / length)
    factor = 1.0 / math.sqrt(length)
    return (jnp.cos(angle) * factor, jnp.sin(angle) * factor)


def lon_forward_table(cos_table, sin_table, ndev):
    share = cos_table.shape[1] // ndev
    cos_g = cos_table.reshape(-1, ndev, 1, share)
    sin_g = -sin_table.reshape(-1, ndev, 1, share)
    return jnp.concatenate([cos_g, sin_g], axis=2).reshape(cos_table.shape[0], -1)


def lon_forward(field, table):
    values = field.astype(jnp.float32)
    return jnp.einsum("ibln,nc->iblc", values, table, precision=HIGHEST)


def lat_forward(spectrum, cos_table, sin_table):
    top = jnp.stack([cos_table, sin_table], axis=1)
    bottom = jnp.stack([-sin_table, cos_table], axis=1)
    table = jnp.stack([top, bottom])
    return jnp.einsum("ofpl,iblpj->oibfj", table, spectrum, precision=HIGHEST)


def lat_inverse(spectrum, cos_table, sin_table):
    top = jnp.stack([cos_table, -sin_table])
    bottom = jnp.stack([sin_table, cos_table])
    table = jnp.stack([top, bottom])
    return jnp.einsum("opfl,pibfj->oiblj", table, spectrum, precision=HIGHEST)


def lon_inverse(spectrum, cos_table, sin_table):
    table = jnp.stack([cos_table, -sin_table])
    return jnp.einsum("piblk,pnk->ibln", spectrum, table, precision=HIGHEST)


def mode_mask(signed, wavenumber, keep_lon, keep_lat):
    lat_kept = (signed >= -keep_lat) & (signed < keep_lat)
    lon_kept = wavenumber < keep_lon
    factor = jnp.where(wavenumber == 0, 1.0, 2.0).astype(jnp.float32)
    return (lat_kept[:, None] & lon_kept[None, :]).astype(jnp.float32) * factor[None, :]


def block_product(weights, values):
    return jnp.einsum("kij,kjm->kim", weights, values, precision=HIGHEST)


def complex_apply(weights, values):
    real_part = block_product(weights[0], values[0]) - block_product(weights[1], values[1])
    imag_part = block_product(weights[1], values[0]) + block_product(weights[0], values[1])
    return jnp.stack([real_part, imag_part])


def complex_adjoint(weights, values):
    real_t = jnp.swapaxes(weights[0], 1, 2)
    imag_t = jnp.swapaxes(weights[1], 1, 2)
    real_part = block_product(real_t, values[0]) + block_product(imag_t, values[1])
    imag_part = block_product(real_t, values[1]) - block_product(imag_t, values[0])
    return jnp.stack([real_part, imag_part])


def complex_outer(left, right):

    def outer(first, second):
        return jnp.einsum("kim,kjm->kij", first, second, precision=HIGHEST)

    real_part = outer(left[0], right[0]) + outer(left[1], right[1])
    imag_part = outer(left[1], right[0]) - outer(left[0], right[1])
    return jnp.stack([real_part, imag_part])


def gelu_pair(values):
    inner = 0.7978845608 * (values + 0.044715 * values * values * values)
    tangent = jnp.tanh(inner)
    output = 0.5 * values * (1.0 + tangent)
    slope = 0.5 * (1.0 + tangent) + 0.5 * values * (1.0 - tangent * tangent) * 0.7978845608 * (
        1.0 + 3.0 * 0.044715 * values * values
    )
    return (output, slope)


def backprop(spectrum, grad_spec, weight_in, bias_in, weight_out):
    before = complex_apply(weight_in, spectrum) + bias_in[..., None]
    hidden, slope = gelu_pair(before)
    grad_hidden = complex_adjoint(weight_out, grad_spec)
    grad_before = grad_hidden * slope
    grad_modes = complex_adjoint(weight_in, grad_before)
    grad_w_out = complex_outer(grad_spec, hidden)
    grad_w_in = complex_outer(grad_before, spectrum)
    return (
        grad_modes,
        grad_w_in,
        jnp.sum(grad_before, axis=-1),
        grad_w_out,
        jnp.sum(grad_spec, axis=-1),
    )


SPACE = ("sx", "sy", "sc")


def exchange(values, axis):
    values = lax.all_to_all(values, SPACE[1:], split_axis=axis + 1, concat_axis=axis + 1, tiled=True)
    return lax.all_to_all(values, SPACE[0], split_axis=axis, concat_axis=axis, tiled=True)


def to_columns(spectrum, groups):
    nblocks, width, rows, _ = spectrum.shape
    split = spectrum.reshape(nblocks, width, rows, groups[0], groups[1], -1)
    moved = exchange(split, 3)
    moved = jnp.moveaxis(moved, 2, 4)
    return moved.reshape(nblocks, width, groups[0] * groups[1] * rows, 2, -1)


def sum_over(flat, axis):
    n = lax.axis_size(axis)
    pad = (-flat.shape[0]) % n
    pieces = jnp.pad(flat, (0, pad)).reshape(n, -1)
    got = lax.all_to_all(pieces, axis, split_axis=0, concat_axis=0, tiled=True)
    mine = jnp.sum(got, axis=0)
    spread = jnp.broadcast_to(mine[None], pieces.shape)
    full = lax.all_to_all(spread, axis, split_axis=0, concat_axis=0, tiled=True)
    return full.reshape(-1)[: flat.shape[0]]


def shards(activations, cotangent, kept_modes, weight_in, bias_in, weight_out):
    field = activations[0]
    own_grad = cotangent[0]
    nblocks = field.shape[0]
    width = field.shape[1]
    groups = (lax.axis_size(SPACE[0]), lax.axis_size(SPACE[1:]))
    ndev = groups[0] * groups[1]
    received = from_behind(own_grad, "pipe", -1)
    section_index = lax.axis_index("pipe")
    last_section = lax.axis_size("pipe") - 1
    lon_cos, lon_sin = lon_tables(LON, KEEP_LON)
    lat_cos, lat_sin = lat_tables(LAT, KEEP_LAT)
    table = lon_forward_table(lon_cos, lon_sin, ndev)
    col_field = to_columns(lon_forward(field, table), groups)
    spectrum = lat_forward(col_field, lat_cos, lat_sin)
    spectrum, received = lax.optimization_barrier((spectrum, received))
    upstream = jnp.where(section_index == last_section, own_grad, received)
    col_grad = to_columns(lon_forward(upstream, table), groups)
    grad_spec = lat_forward(col_grad, lat_cos, lat_sin)
    share = KEEP_LON // ndev
    signed = jnp.arange(2 * KEEP_LAT, dtype=jnp.int32) - KEEP_LAT
    wavenumber = lax.axis_index(SPACE) * share + jnp.arange(share, dtype=jnp.int32)
    weight = mode_mask(signed, wavenumber, kept_modes[0, 0], kept_modes[0, 1])
    grad_spec = grad_spec * weight
    spectrum = spectrum.reshape(2, nblocks, width, -1)
    grad_spec = grad_spec.reshape(2, nblocks, width, -1)
    grad_modes, grad_w_in, grad_b_in, grad_w_out, grad_b_out = backprop(
        spectrum, grad_spec, weight_in[0], bias_in[0], weight_out[0]
    )
    grad_modes = grad_modes.reshape(2, nblocks, width, 2 * KEEP_LAT, share)
    lat_back = lat_inverse(grad_modes, lat_cos, lat_sin)
    parts = (grad_w_in, grad_b_in, grad_w_out, grad_b_out)
    flat = jnp.concatenate([p.reshape(-1) for p in parts])
    pad = (-flat.shape[0]) % ndev
    pieces = jnp.pad(flat, (0, pad)).reshape(ndev, -1)
    rows = LAT // ndev
    back = lat_back.reshape(2, nblocks, width, ndev, rows, share)
    back = jnp.moveaxis(back, 3, 0).reshape(ndev, -1)
    joined = jnp.concatenate([back, pieces], axis=1).reshape(groups[0], groups[1], -1)
    moved = exchange(joined, 0).reshape(ndev, -1)
    rows_back = moved[:, : back.shape[1]].reshape(ndev, 2, nblocks, width, rows, share)
    rows_back = jnp.moveaxis(rows_back, 0, 4).reshape(2, nblocks, width, rows, ndev * share)
    mine = jnp.sum(moved[:, back.shape[1]:], axis=0)
    spread = jnp.broadcast_to(mine[None], pieces.shape)
    flat = exchange(spread.reshape(groups[0], groups[1], -1), 0)
    flat = flat.reshape(-1)[: flat.size - pad]
    inverse = lon_inverse(rows_back, lon_cos, lon_sin)
    factor = 1.0 / math.sqrt(2 * KEEP_LAT * KEEP_LON)
    flat = flat * factor
    sums = []
    start = 0
    for p in parts:
        sums.append(flat[start:start + p.size].reshape(p.shape)[None])
        start += p.size
    grad_field = (upstream.astype(jnp.float32) + inverse).astype(jnp.bfloat16)
    return (grad_field[None], *sums)


def solution(mesh):
    inner = {"sy": 8, "sc": 2}
    size = mesh.shape["space"]
    fine = Mesh(
        mesh.devices.reshape(mesh.shape["pipe"], size // 16, inner["sy"], inner["sc"]),
        ("pipe",) + SPACE,
    )
    return jax.shard_map(
        shards,
        mesh=fine,
        in_specs=(
            P("pipe", None, None, SPACE, None),
            P("pipe", None, None, SPACE, None),
            P("pipe", None),
            P("pipe", None, None, None, None),
            P("pipe", None, None, None),
            P("pipe", None, None, None, None),
        ),
        out_specs=(
            P("pipe", None, None, SPACE, None),
            P("pipe", None, None, None, None),
            P("pipe", None, None, None),
            P("pipe", None, None, None, None),
            P("pipe", None, None, None),
        ),
        check_vma=False,
    )
```

```python
import math

import jax
import jax.numpy as jnp
from jax import lax
from jax.sharding import PartitionSpec as P

LAT = 256
LON = 512
KEEP_LON = 128
KEEP_LAT = 64


HIGHEST = lax.Precision.HIGH


def from_behind(block, axis, distance):
    devices = range(lax.axis_size(axis))
    route = [(i - distance, i) for i in devices if i - distance in devices]
    return lax.ppermute(block, axis, route)


def lon_tables(length, count):
    column = jnp.arange(length, dtype=jnp.int32)
    number = jnp.arange(count, dtype=jnp.int32)
    phase = column[:, None] * number[None, :] % length
    angle = phase.astype(jnp.float32) * (2.0 * math.pi / length)
    factor = 1.0 / math.sqrt(length)
    return (jnp.cos(angle) * factor, jnp.sin(angle) * factor)


def lat_tables(length, half):
    signed = jnp.arange(2 * half, dtype=jnp.int32) - half
    row_index = jnp.arange(length, dtype=jnp.int32)
    phase = signed[:, None] * row_index[None, :] % length
    angle = phase.astype(jnp.float32) * (2.0 * math.pi / length)
    factor = 1.0 / math.sqrt(length)
    return (jnp.cos(angle) * factor, jnp.sin(angle) * factor)


def lon_forward_table(cos_table, sin_table, ndev):
    share = cos_table.shape[1] // ndev
    cos_g = cos_table.reshape(-1, ndev, 1, share)
    sin_g = -sin_table.reshape(-1, ndev, 1, share)
    return jnp.concatenate([cos_g, sin_g], axis=2).reshape(cos_table.shape[0], -1)


def lon_forward(field, table):
    values = field.astype(jnp.float32)
    return jnp.einsum("ibln,nc->iblc", values, table, precision=HIGHEST)


def lat_forward(spectrum, cos_table, sin_table):
    top = jnp.stack([cos_table, sin_table], axis=1)
    bottom = jnp.stack([-sin_table, cos_table], axis=1)
    table = jnp.stack([top, bottom])
    return jnp.einsum("ofpl,iblpj->oibfj", table, spectrum, precision=HIGHEST)


def lat_inverse(spectrum, cos_table, sin_table):
    top = jnp.stack([cos_table, -sin_table])
    bottom = jnp.stack([sin_table, cos_table])
    table = jnp.stack([top, bottom])
    return jnp.einsum("opfl,pibfj->oiblj", table, spectrum, precision=HIGHEST)


def lon_inverse(spectrum, cos_table, sin_table):
    table = jnp.stack([cos_table, -sin_table])
    return jnp.einsum("piblk,pnk->ibln", spectrum, table, precision=HIGHEST)


def mode_mask(signed, wavenumber, keep_lon, keep_lat):
    lat_kept = (signed >= -keep_lat) & (signed < keep_lat)
    lon_kept = wavenumber < keep_lon
    factor = jnp.where(wavenumber == 0, 1.0, 2.0).astype(jnp.float32)
    return (lat_kept[:, None] & lon_kept[None, :]).astype(jnp.float32) * factor[None, :]


def block_product(weights, values):
    return jnp.einsum("kij,kjm->kim", weights, values, precision=HIGHEST)


def complex_apply(weights, values):
    real_part = block_product(weights[0], values[0]) - block_product(weights[1], values[1])
    imag_part = block_product(weights[1], values[0]) + block_product(weights[0], values[1])
    return jnp.stack([real_part, imag_part])


def complex_adjoint(weights, values):
    real_t = jnp.swapaxes(weights[0], 1, 2)
    imag_t = jnp.swapaxes(weights[1], 1, 2)
    real_part = block_product(real_t, values[0]) + block_product(imag_t, values[1])
    imag_part = block_product(real_t, values[1]) - block_product(imag_t, values[0])
    return jnp.stack([real_part, imag_part])


def complex_outer(left, right):

    def outer(first, second):
        return jnp.einsum("kim,kjm->kij", first, second, precision=HIGHEST)

    real_part = outer(left[0], right[0]) + outer(left[1], right[1])
    imag_part = outer(left[1], right[0]) - outer(left[0], right[1])
    return jnp.stack([real_part, imag_part])


def gelu_pair(values):
    inner = 0.7978845608 * (values + 0.044715 * values * values * values)
    tangent = jnp.tanh(inner)
    output = 0.5 * values * (1.0 + tangent)
    slope = 0.5 * (1.0 + tangent) + 0.5 * values * (1.0 - tangent * tangent) * 0.7978845608 * (
        1.0 + 3.0 * 0.044715 * values * values
    )
    return (output, slope)


def backprop(spectrum, grad_spec, weight_in, bias_in, weight_out):
    before = complex_apply(weight_in, spectrum) + bias_in[..., None]
    hidden, slope = gelu_pair(before)
    grad_hidden = complex_adjoint(weight_out, grad_spec)
    grad_before = grad_hidden * slope
    grad_modes = complex_adjoint(weight_in, grad_before)
    grad_w_out = complex_outer(grad_spec, hidden)
    grad_w_in = complex_outer(grad_before, spectrum)
    return (
        grad_modes,
        grad_w_in,
        jnp.sum(grad_before, axis=-1),
        grad_w_out,
        jnp.sum(grad_spec, axis=-1),
    )


def to_columns(spectrum, ndev):
    moved = lax.all_to_all(spectrum, "space", split_axis=3, concat_axis=2, tiled=True)
    nblocks, width, rows, _ = moved.shape
    return moved.reshape(nblocks, width, rows, 2, -1)


def sum_over(flat, axis):
    n = lax.axis_size(axis)
    pad = (-flat.shape[0]) % n
    pieces = jnp.pad(flat, (0, pad)).reshape(n, -1)
    got = lax.all_to_all(pieces, axis, split_axis=0, concat_axis=0, tiled=True)
    mine = jnp.sum(got, axis=0)
    spread = jnp.broadcast_to(mine[None], pieces.shape)
    full = lax.all_to_all(spread, axis, split_axis=0, concat_axis=0, tiled=True)
    return full.reshape(-1)[: flat.shape[0]]


def shards(activations, cotangent, kept_modes, weight_in, bias_in, weight_out):
    field = activations[0]
    own_grad = cotangent[0]
    nblocks = field.shape[0]
    width = field.shape[1]
    ndev = lax.axis_size("space")
    received = from_behind(own_grad, "pipe", -1)
    section_index = lax.axis_index("pipe")
    last_section = lax.axis_size("pipe") - 1
    lon_cos, lon_sin = lon_tables(LON, KEEP_LON)
    lat_cos, lat_sin = lat_tables(LAT, KEEP_LAT)
    table = lon_forward_table(lon_cos, lon_sin, ndev)
    upstream = jnp.where(section_index == last_section, own_grad, received)
    both = jnp.concatenate([lon_forward(field, table), lon_forward(upstream, table)])
    columns = to_columns(both, ndev)
    spectrum = lat_forward(columns[:nblocks], lat_cos, lat_sin)
    grad_spec = lat_forward(columns[nblocks:], lat_cos, lat_sin)
    share = KEEP_LON // ndev
    signed = jnp.arange(2 * KEEP_LAT, dtype=jnp.int32) - KEEP_LAT
    wavenumber = lax.axis_index("space") * share + jnp.arange(share, dtype=jnp.int32)
    weight = mode_mask(signed, wavenumber, kept_modes[0, 0], kept_modes[0, 1])
    grad_spec = grad_spec * weight
    spectrum = spectrum.reshape(2, nblocks, width, -1)
    grad_spec = grad_spec.reshape(2, nblocks, width, -1)
    grad_modes, grad_w_in, grad_b_in, grad_w_out, grad_b_out = backprop(
        spectrum, grad_spec, weight_in[0], bias_in[0], weight_out[0]
    )
    grad_modes = grad_modes.reshape(2, nblocks, width, 2 * KEEP_LAT, share)
    lat_back = lat_inverse(grad_modes, lat_cos, lat_sin)
    parts = (grad_w_in, grad_b_in, grad_w_out, grad_b_out)
    flat = jnp.concatenate([p.reshape(-1) for p in parts])
    pad = (-flat.shape[0]) % ndev
    pieces = jnp.pad(flat, (0, pad)).reshape(ndev, -1)
    rows = LAT // ndev
    back = lat_back.reshape(2, nblocks, width, ndev, rows, share)
    back = jnp.moveaxis(back, 3, 0).reshape(ndev, -1)
    moved = lax.all_to_all(
        jnp.concatenate([back, pieces], axis=1), "space", split_axis=0, concat_axis=0, tiled=True
    )
    rows_back = moved[:, : back.shape[1]].reshape(ndev, 2, nblocks, width, rows, share)
    rows_back = jnp.moveaxis(rows_back, 0, 4).reshape(2, nblocks, width, rows, ndev * share)
    mine = jnp.sum(moved[:, back.shape[1]:], axis=0)
    spread = jnp.broadcast_to(mine[None], pieces.shape)
    flat = lax.all_to_all(spread, "space", split_axis=0, concat_axis=0, tiled=True)
    flat = flat.reshape(-1)[: flat.size - pad]
    inverse = lon_inverse(rows_back, lon_cos, lon_sin)
    factor = 1.0 / math.sqrt(2 * KEEP_LAT * KEEP_LON)
    flat = flat * factor
    sums = []
    start = 0
    for p in parts:
        sums.append(flat[start:start + p.size].reshape(p.shape)[None])
        start += p.size
    grad_field = (upstream.astype(jnp.float32) + inverse).astype(jnp.bfloat16)
    return (grad_field[None], *sums)


def solution(mesh):
    return jax.shard_map(
        shards,
        mesh=mesh,
        in_specs=(
            P("pipe", None, None, "space", None),
            P("pipe", None, None, "space", None),
            P("pipe", None),
            P("pipe", None, None, None, None),
            P("pipe", None, None, None),
            P("pipe", None, None, None, None),
        ),
        out_specs=(
            P("pipe", None, None, "space", None),
            P("pipe", None, None, None, None),
            P("pipe", None, None, None),
            P("pipe", None, None, None, None),
            P("pipe", None, None, None),
        ),
        check_vma=False,
    )
```

```python
import math

import jax
import jax.numpy as jnp
from jax import lax
from jax.sharding import PartitionSpec as P

LAT = 256
LON = 512
KEEP_LON = 128
KEEP_LAT = 64


HIGHEST = lax.Precision.HIGH


def from_behind(block, axis, distance):
    devices = range(lax.axis_size(axis))
    route = [(i - distance, i) for i in devices if i - distance in devices]
    return lax.ppermute(block, axis, route)


def lon_tables(length, count):
    column = jnp.arange(length, dtype=jnp.int32)
    number = jnp.arange(count, dtype=jnp.int32)
    phase = column[:, None] * number[None, :] % length
    angle = phase.astype(jnp.float32) * (2.0 * math.pi / length)
    factor = 1.0 / math.sqrt(length)
    return (jnp.cos(angle) * factor, jnp.sin(angle) * factor)


def lat_tables(length, half):
    signed = jnp.arange(2 * half, dtype=jnp.int32) - half
    row_index = jnp.arange(length, dtype=jnp.int32)
    phase = signed[:, None] * row_index[None, :] % length
    angle = phase.astype(jnp.float32) * (2.0 * math.pi / length)
    factor = 1.0 / math.sqrt(length)
    return (jnp.cos(angle) * factor, jnp.sin(angle) * factor)


def lon_forward_table(cos_table, sin_table, ndev):
    share = cos_table.shape[1] // ndev
    cos_g = cos_table.reshape(-1, ndev, 1, share)
    sin_g = -sin_table.reshape(-1, ndev, 1, share)
    return jnp.concatenate([cos_g, sin_g], axis=2).reshape(cos_table.shape[0], -1)


def lon_forward(field, table):
    values = field.astype(jnp.float32)
    return jnp.einsum("ibln,nc->iblc", values, table, precision=HIGHEST)


def lat_forward(spectrum, cos_table, sin_table):
    top = jnp.stack([cos_table, sin_table], axis=1)
    bottom = jnp.stack([-sin_table, cos_table], axis=1)
    table = jnp.stack([top, bottom])
    return jnp.einsum("ofpl,iblpj->oibfj", table, spectrum, precision=HIGHEST)


def lat_inverse(spectrum, cos_table, sin_table):
    top = jnp.stack([cos_table, -sin_table])
    bottom = jnp.stack([sin_table, cos_table])
    table = jnp.stack([top, bottom])
    return jnp.einsum("opfl,pibfj->oiblj", table, spectrum, precision=HIGHEST)


def lon_inverse(spectrum, cos_table, sin_table):
    table = jnp.stack([cos_table, -sin_table])
    return jnp.einsum("piblk,pnk->ibln", spectrum, table, precision=HIGHEST)


def mode_mask(signed, wavenumber, keep_lon, keep_lat):
    lat_kept = (signed >= -keep_lat) & (signed < keep_lat)
    lon_kept = wavenumber < keep_lon
    factor = jnp.where(wavenumber == 0, 1.0, 2.0).astype(jnp.float32)
    return (lat_kept[:, None] & lon_kept[None, :]).astype(jnp.float32) * factor[None, :]


def block_product(weights, values):
    return jnp.einsum("kij,kjm->kim", weights, values, precision=HIGHEST)


def complex_apply(weights, values):
    real_part = block_product(weights[0], values[0]) - block_product(weights[1], values[1])
    imag_part = block_product(weights[1], values[0]) + block_product(weights[0], values[1])
    return jnp.stack([real_part, imag_part])


def complex_adjoint(weights, values):
    real_t = jnp.swapaxes(weights[0], 1, 2)
    imag_t = jnp.swapaxes(weights[1], 1, 2)
    real_part = block_product(real_t, values[0]) + block_product(imag_t, values[1])
    imag_part = block_product(real_t, values[1]) - block_product(imag_t, values[0])
    return jnp.stack([real_part, imag_part])


def complex_outer(left, right):

    def outer(first, second):
        return jnp.einsum("kim,kjm->kij", first, second, precision=HIGHEST)

    real_part = outer(left[0], right[0]) + outer(left[1], right[1])
    imag_part = outer(left[1], right[0]) - outer(left[0], right[1])
    return jnp.stack([real_part, imag_part])


def gelu_pair(values):
    inner = 0.7978845608 * (values + 0.044715 * values * values * values)
    tangent = jnp.tanh(inner)
    output = 0.5 * values * (1.0 + tangent)
    slope = 0.5 * (1.0 + tangent) + 0.5 * values * (1.0 - tangent * tangent) * 0.7978845608 * (
        1.0 + 3.0 * 0.044715 * values * values
    )
    return (output, slope)


def backprop(spectrum, grad_spec, weight_in, bias_in, weight_out):
    before = complex_apply(weight_in, spectrum) + bias_in[..., None]
    hidden, slope = gelu_pair(before)
    grad_hidden = complex_adjoint(weight_out, grad_spec)
    grad_before = grad_hidden * slope
    grad_modes = complex_adjoint(weight_in, grad_before)
    grad_w_out = complex_outer(grad_spec, hidden)
    grad_w_in = complex_outer(grad_before, spectrum)
    return (
        grad_modes,
        grad_w_in,
        jnp.sum(grad_before, axis=-1),
        grad_w_out,
        jnp.sum(grad_spec, axis=-1),
    )


def to_columns(spectrum, ndev):
    moved = lax.all_to_all(spectrum, "space", split_axis=3, concat_axis=2, tiled=True)
    nblocks, width, rows, _ = moved.shape
    return moved.reshape(nblocks, width, rows, 2, -1)


def sum_over(flat, axis):
    n = lax.axis_size(axis)
    pad = (-flat.shape[0]) % n
    pieces = jnp.pad(flat, (0, pad)).reshape(n, -1)
    got = lax.all_to_all(pieces, axis, split_axis=0, concat_axis=0, tiled=True)
    mine = jnp.sum(got, axis=0)
    spread = jnp.broadcast_to(mine[None], pieces.shape)
    full = lax.all_to_all(spread, axis, split_axis=0, concat_axis=0, tiled=True)
    return full.reshape(-1)[: flat.shape[0]]


def shards(activations, cotangent, kept_modes, weight_in, bias_in, weight_out):
    field = activations[0]
    own_grad = cotangent[0]
    nblocks = field.shape[0]
    width = field.shape[1]
    ndev = lax.axis_size("space")
    received = from_behind(own_grad, "pipe", -1)
    section_index = lax.axis_index("pipe")
    last_section = lax.axis_size("pipe") - 1
    lon_cos, lon_sin = lon_tables(LON, KEEP_LON)
    lat_cos, lat_sin = lat_tables(LAT, KEEP_LAT)
    table = lon_forward_table(lon_cos, lon_sin, ndev)
    col_field = to_columns(lon_forward(field, table), ndev)
    spectrum = lat_forward(col_field, lat_cos, lat_sin)
    spectrum, received = lax.optimization_barrier((spectrum, received))
    upstream = jnp.where(section_index == last_section, own_grad, received)
    share = KEEP_LON // ndev
    signed = jnp.arange(2 * KEEP_LAT, dtype=jnp.int32) - KEEP_LAT
    wavenumber = lax.axis_index("space") * share + jnp.arange(share, dtype=jnp.int32)
    weight = mode_mask(signed, wavenumber, kept_modes[0, 0], kept_modes[0, 1])
    rows = LAT // ndev
    factor = 1.0 / math.sqrt(2 * KEEP_LAT * KEEP_LON)
    fields = []
    mine = []
    layouts = []
    for b in range(nblocks):
        one = slice(b, b + 1)
        col_grad = to_columns(lon_forward(upstream[one], table), ndev)
        grad_spec = lat_forward(col_grad, lat_cos, lat_sin) * weight
        grad_modes, grad_w_in, grad_b_in, grad_w_out, grad_b_out = backprop(
            spectrum[:, one].reshape(2, 1, width, -1),
            grad_spec.reshape(2, 1, width, -1),
            weight_in[0][:, one],
            bias_in[0][:, one],
            weight_out[0][:, one],
        )
        grad_modes = grad_modes.reshape(2, 1, width, 2 * KEEP_LAT, share)
        lat_back = lat_inverse(grad_modes, lat_cos, lat_sin)
        parts = (grad_w_in, grad_b_in, grad_w_out, grad_b_out)
        flat = jnp.concatenate([p.reshape(-1) for p in parts])
        pad = (-flat.shape[0]) % ndev
        pieces = jnp.pad(flat, (0, pad)).reshape(ndev, -1)
        back = lat_back.reshape(2, 1, width, ndev, rows, share)
        back = jnp.moveaxis(back, 3, 0).reshape(ndev, -1)
        moved = lax.all_to_all(
            jnp.concatenate([back, pieces], axis=1), "space", split_axis=0, concat_axis=0, tiled=True
        )
        rows_back = moved[:, : back.shape[1]].reshape(ndev, 2, 1, width, rows, share)
        rows_back = jnp.moveaxis(rows_back, 0, 4).reshape(2, 1, width, rows, ndev * share)
        mine.append(jnp.sum(moved[:, back.shape[1]:], axis=0))
        layouts.append(([p.shape for p in parts], flat.shape[0]))
        inverse = lon_inverse(rows_back, lon_cos, lon_sin)
        fields.append((upstream[one].astype(jnp.float32) + inverse).astype(jnp.bfloat16))
    joined = jnp.concatenate(mine)
    spread = jnp.broadcast_to(joined[None], (ndev, joined.shape[0]))
    full = lax.all_to_all(spread, "space", split_axis=0, concat_axis=0, tiled=True) * factor
    width_b = joined.shape[0] // nblocks
    grads = [[], [], [], []]
    for b in range(nblocks):
        shapes, size = layouts[b]
        flat = full[:, b * width_b:(b + 1) * width_b].reshape(-1)[:size]
        start = 0
        for n, shape in enumerate(shapes):
            count = math.prod(shape)
            grads[n].append(flat[start:start + count].reshape(shape))
            start += count
    sums = [jnp.concatenate(g, axis=1)[None] for g in grads]
    grad_field = jnp.concatenate(fields)
    return (grad_field[None], *sums)


def solution(mesh):
    return jax.shard_map(
        shards,
        mesh=mesh,
        in_specs=(
            P("pipe", None, None, "space", None),
            P("pipe", None, None, "space", None),
            P("pipe", None),
            P("pipe", None, None, None, None),
            P("pipe", None, None, None),
            P("pipe", None, None, None, None),
        ),
        out_specs=(
            P("pipe", None, None, "space", None),
            P("pipe", None, None, None, None),
            P("pipe", None, None, None),
            P("pipe", None, None, None, None),
            P("pipe", None, None, None),
        ),
        check_vma=False,
    )
```

```python
import math

import jax
import jax.numpy as jnp
from jax import lax
from jax.sharding import PartitionSpec as P

LAT = 256
LON = 512
KEEP_LON = 128
KEEP_LAT = 64


HIGHEST = lax.Precision.HIGH


def from_behind(block, axis, distance):
    devices = range(lax.axis_size(axis))
    route = [(i - distance, i) for i in devices if i - distance in devices]
    return lax.ppermute(block, axis, route)


def lon_tables(length, count):
    column = jnp.arange(length, dtype=jnp.int32)
    number = jnp.arange(count, dtype=jnp.int32)
    phase = column[:, None] * number[None, :] % length
    angle = phase.astype(jnp.float32) * (2.0 * math.pi / length)
    factor = 1.0 / math.sqrt(length)
    return (jnp.cos(angle) * factor, jnp.sin(angle) * factor)


def lat_tables(length, half):
    signed = jnp.arange(2 * half, dtype=jnp.int32) - half
    row_index = jnp.arange(length, dtype=jnp.int32)
    phase = signed[:, None] * row_index[None, :] % length
    angle = phase.astype(jnp.float32) * (2.0 * math.pi / length)
    factor = 1.0 / math.sqrt(length)
    return (jnp.cos(angle) * factor, jnp.sin(angle) * factor)


def lon_forward_table(cos_table, sin_table, ndev):
    share = cos_table.shape[1] // ndev
    cos_g = cos_table.reshape(-1, ndev, 1, share)
    sin_g = -sin_table.reshape(-1, ndev, 1, share)
    return jnp.concatenate([cos_g, sin_g], axis=2).reshape(cos_table.shape[0], -1)


def lon_forward(field, table):
    values = field.astype(jnp.float32)
    return jnp.einsum("ibln,nc->iblc", values, table, precision=HIGHEST)


def lat_forward(spectrum, cos_table, sin_table):
    top = jnp.stack([cos_table, sin_table], axis=1)
    bottom = jnp.stack([-sin_table, cos_table], axis=1)
    table = jnp.stack([top, bottom])
    return jnp.einsum("ofpl,iblpj->oibfj", table, spectrum, precision=HIGHEST)


def lat_inverse(spectrum, cos_table, sin_table):
    top = jnp.stack([cos_table, -sin_table])
    bottom = jnp.stack([sin_table, cos_table])
    table = jnp.stack([top, bottom])
    return jnp.einsum("opfl,pibfj->oiblj", table, spectrum, precision=HIGHEST)


def lon_inverse(spectrum, cos_table, sin_table):
    table = jnp.stack([cos_table, -sin_table])
    return jnp.einsum("piblk,pnk->ibln", spectrum, table, precision=HIGHEST)


def lat_inverse_split(spectrum, cos_table, sin_table, ndev):
    top = jnp.stack([cos_table, -sin_table])
    bottom = jnp.stack([sin_table, cos_table])
    table = jnp.stack([top, bottom])
    table = table.reshape(table.shape[:3] + (ndev, -1))
    return jnp.einsum("opfdr,pibfj->doibrj", table, spectrum, precision=HIGHEST)


def lon_inverse_split(spectrum, cos_table, sin_table, ndev):
    table = jnp.stack([cos_table, -sin_table])
    table = table.reshape(table.shape[:2] + (ndev, -1))
    return jnp.einsum("dpiblj,pndj->ibln", spectrum, table, precision=HIGHEST)


def mode_mask(signed, wavenumber, keep_lon, keep_lat):
    lat_kept = (signed >= -keep_lat) & (signed < keep_lat)
    lon_kept = wavenumber < keep_lon
    factor = jnp.where(wavenumber == 0, 1.0, 2.0).astype(jnp.float32)
    return (lat_kept[:, None] & lon_kept[None, :]).astype(jnp.float32) * factor[None, :]


def block_product(weights, values):
    return jnp.einsum("kij,kjm->kim", weights, values, precision=HIGHEST)


def complex_apply(weights, values):
    real_part = block_product(weights[0], values[0]) - block_product(weights[1], values[1])
    imag_part = block_product(weights[1], values[0]) + block_product(weights[0], values[1])
    return jnp.stack([real_part, imag_part])


def complex_adjoint(weights, values):
    real_t = jnp.swapaxes(weights[0], 1, 2)
    imag_t = jnp.swapaxes(weights[1], 1, 2)
    real_part = block_product(real_t, values[0]) + block_product(imag_t, values[1])
    imag_part = block_product(real_t, values[1]) - block_product(imag_t, values[0])
    return jnp.stack([real_part, imag_part])


def complex_outer(left, right):

    def outer(first, second):
        return jnp.einsum("kim,kjm->kij", first, second, precision=HIGHEST)

    real_part = outer(left[0], right[0]) + outer(left[1], right[1])
    imag_part = outer(left[1], right[0]) - outer(left[0], right[1])
    return jnp.stack([real_part, imag_part])


def gelu_pair(values):
    inner = 0.7978845608 * (values + 0.044715 * values * values * values)
    tangent = jnp.tanh(inner)
    output = 0.5 * values * (1.0 + tangent)
    slope = 0.5 * (1.0 + tangent) + 0.5 * values * (1.0 - tangent * tangent) * 0.7978845608 * (
        1.0 + 3.0 * 0.044715 * values * values
    )
    return (output, slope)


def backprop(spectrum, grad_spec, weight_in, bias_in, weight_out):
    before = complex_apply(weight_in, spectrum) + bias_in[..., None]
    hidden, slope = gelu_pair(before)
    grad_hidden = complex_adjoint(weight_out, grad_spec)
    grad_before = grad_hidden * slope
    grad_modes = complex_adjoint(weight_in, grad_before)
    grad_w_out = complex_outer(grad_spec, hidden)
    grad_w_in = complex_outer(grad_before, spectrum)
    return (
        grad_modes,
        grad_w_in,
        jnp.sum(grad_before, axis=-1),
        grad_w_out,
        jnp.sum(grad_spec, axis=-1),
    )


def to_columns(spectrum, ndev):
    moved = lax.all_to_all(spectrum, "space", split_axis=3, concat_axis=2, tiled=True)
    nblocks, width, rows, _ = moved.shape
    return moved.reshape(nblocks, width, rows, 2, -1)


def sum_over(flat, axis):
    n = lax.axis_size(axis)
    pad = (-flat.shape[0]) % n
    pieces = jnp.pad(flat, (0, pad)).reshape(n, -1)
    got = lax.all_to_all(pieces, axis, split_axis=0, concat_axis=0, tiled=True)
    mine = jnp.sum(got, axis=0)
    spread = jnp.broadcast_to(mine[None], pieces.shape)
    full = lax.all_to_all(spread, axis, split_axis=0, concat_axis=0, tiled=True)
    return full.reshape(-1)[: flat.shape[0]]


def shards(activations, cotangent, kept_modes, weight_in, bias_in, weight_out):
    field = activations[0]
    own_grad = cotangent[0]
    nblocks = field.shape[0]
    width = field.shape[1]
    ndev = lax.axis_size("space")
    received = from_behind(own_grad, "pipe", -1)
    section_index = lax.axis_index("pipe")
    last_section = lax.axis_size("pipe") - 1
    lon_cos, lon_sin = lon_tables(LON, KEEP_LON)
    lat_cos, lat_sin = lat_tables(LAT, KEEP_LAT)
    table = lon_forward_table(lon_cos, lon_sin, ndev)
    col_field = to_columns(lon_forward(field, table), ndev)
    col_field, received = lax.optimization_barrier((col_field, received))
    spectrum = lat_forward(col_field, lat_cos, lat_sin)
    upstream = jnp.where(section_index == last_section, own_grad, received)
    col_grad = to_columns(lon_forward(upstream, table), ndev)
    grad_spec = lat_forward(col_grad, lat_cos, lat_sin)
    share = KEEP_LON // ndev
    signed = jnp.arange(2 * KEEP_LAT, dtype=jnp.int32) - KEEP_LAT
    wavenumber = lax.axis_index("space") * share + jnp.arange(share, dtype=jnp.int32)
    weight = mode_mask(signed, wavenumber, kept_modes[0, 0], kept_modes[0, 1])
    grad_spec = grad_spec * weight
    spectrum = spectrum.reshape(2, nblocks, width, -1)
    grad_spec = grad_spec.reshape(2, nblocks, width, -1)
    grad_modes, grad_w_in, grad_b_in, grad_w_out, grad_b_out = backprop(
        spectrum, grad_spec, weight_in[0], bias_in[0], weight_out[0]
    )
    grad_modes = grad_modes.reshape(2, nblocks, width, 2 * KEEP_LAT, share)
    rows = LAT // ndev
    back = lat_inverse_split(grad_modes, lat_cos, lat_sin, ndev).reshape(ndev, -1)
    parts = (grad_w_in, grad_b_in, grad_w_out, grad_b_out)
    flat = jnp.concatenate([p.reshape(-1) for p in parts])
    pad = (-flat.shape[0]) % ndev
    pieces = jnp.pad(flat, (0, pad)).reshape(ndev, -1)
    moved = lax.all_to_all(
        jnp.concatenate([back, pieces], axis=1), "space", split_axis=0, concat_axis=0, tiled=True
    )
    rows_back = moved[:, : back.shape[1]].reshape(ndev, 2, nblocks, width, rows, share)
    mine = jnp.sum(moved[:, back.shape[1]:], axis=0)
    spread = jnp.broadcast_to(mine[None], pieces.shape)
    flat = lax.all_to_all(spread, "space", split_axis=0, concat_axis=0, tiled=True)
    flat = flat.reshape(-1)[: flat.size - pad]
    inverse = lon_inverse_split(rows_back, lon_cos, lon_sin, ndev)
    factor = 1.0 / math.sqrt(2 * KEEP_LAT * KEEP_LON)
    flat = flat * factor
    sums = []
    start = 0
    for p in parts:
        sums.append(flat[start:start + p.size].reshape(p.shape)[None])
        start += p.size
    grad_field = (upstream.astype(jnp.float32) + inverse).astype(jnp.bfloat16)
    return (grad_field[None], *sums)


def solution(mesh):
    return jax.shard_map(
        shards,
        mesh=mesh,
        in_specs=(
            P("pipe", None, None, "space", None),
            P("pipe", None, None, "space", None),
            P("pipe", None),
            P("pipe", None, None, None, None),
            P("pipe", None, None, None),
            P("pipe", None, None, None, None),
        ),
        out_specs=(
            P("pipe", None, None, "space", None),
            P("pipe", None, None, None, None),
            P("pipe", None, None, None),
            P("pipe", None, None, None, None),
            P("pipe", None, None, None),
        ),
        check_vma=False,
    )
```

```python
import math

import jax
import jax.numpy as jnp
from jax import lax
from jax.sharding import PartitionSpec as P

LAT = 256
LON = 512
KEEP_LON = 128
KEEP_LAT = 64


HIGHEST = lax.Precision.HIGH


def from_behind(block, axis, distance):
    devices = range(lax.axis_size(axis))
    route = [(i - distance, i) for i in devices if i - distance in devices]
    return lax.ppermute(block, axis, route)


def lon_tables(length, count):
    column = jnp.arange(length, dtype=jnp.int32)
    number = jnp.arange(count, dtype=jnp.int32)
    phase = column[:, None] * number[None, :] % length
    angle = phase.astype(jnp.float32) * (2.0 * math.pi / length)
    factor = 1.0 / math.sqrt(length)
    return (jnp.cos(angle) * factor, jnp.sin(angle) * factor)


def lat_tables(length, half):
    signed = jnp.arange(2 * half, dtype=jnp.int32) - half
    row_index = jnp.arange(length, dtype=jnp.int32)
    phase = signed[:, None] * row_index[None, :] % length
    angle = phase.astype(jnp.float32) * (2.0 * math.pi / length)
    factor = 1.0 / math.sqrt(length)
    return (jnp.cos(angle) * factor, jnp.sin(angle) * factor)


def lon_forward_table(cos_table, sin_table, ndev):
    share = cos_table.shape[1] // ndev
    cos_g = cos_table.reshape(-1, ndev, 1, share)
    sin_g = -sin_table.reshape(-1, ndev, 1, share)
    return jnp.concatenate([cos_g, sin_g], axis=2).reshape(cos_table.shape[0], -1)


def lon_forward(field, table):
    values = field.astype(jnp.float32)
    return jnp.einsum("ibln,nc->iblc", values, table, precision=HIGHEST)


def lat_forward(spectrum, cos_table, sin_table):
    top = jnp.stack([cos_table, sin_table], axis=1)
    bottom = jnp.stack([-sin_table, cos_table], axis=1)
    table = jnp.stack([top, bottom])
    return jnp.einsum("ofpl,iblpj->iobfj", table, spectrum, precision=HIGHEST)


def lat_inverse(spectrum, cos_table, sin_table):
    top = jnp.stack([cos_table, -sin_table])
    bottom = jnp.stack([sin_table, cos_table])
    table = jnp.stack([top, bottom])
    return jnp.einsum("opfl,pibfj->oiblj", table, spectrum, precision=HIGHEST)


def lon_inverse(spectrum, cos_table, sin_table):
    table = jnp.stack([cos_table, -sin_table])
    return jnp.einsum("piblk,pnk->ibln", spectrum, table, precision=HIGHEST)


def lat_inverse_split(spectrum, cos_table, sin_table, ndev):
    top = jnp.stack([cos_table, -sin_table])
    bottom = jnp.stack([sin_table, cos_table])
    table = jnp.stack([top, bottom])
    table = table.reshape(table.shape[:3] + (ndev, -1))
    return jnp.einsum("opfdr,ipbfj->doibrj", table, spectrum, precision=HIGHEST)


def lon_inverse_split(spectrum, cos_table, sin_table, ndev):
    table = jnp.stack([cos_table, -sin_table])
    table = table.reshape(table.shape[:2] + (ndev, -1))
    return jnp.einsum("dpiblj,pndj->ibln", spectrum, table, precision=HIGHEST)


def mode_mask(signed, wavenumber, keep_lon, keep_lat):
    lat_kept = (signed >= -keep_lat) & (signed < keep_lat)
    lon_kept = wavenumber < keep_lon
    factor = jnp.where(wavenumber == 0, 1.0, 2.0).astype(jnp.float32)
    return (lat_kept[:, None] & lon_kept[None, :]).astype(jnp.float32) * factor[None, :]


def real_form(weights):
    real_part, imag_part = weights[0], weights[1]
    top = jnp.concatenate([real_part, -imag_part], axis=2)
    bottom = jnp.concatenate([imag_part, real_part], axis=2)
    return jnp.concatenate([top, bottom], axis=1)


def apply(weights, values):
    return jnp.einsum("kij,kjm->kim", weights, values, precision=HIGHEST)


def apply_adjoint(weights, values):
    return jnp.einsum("kji,kjm->kim", weights, values, precision=HIGHEST)


def complex_outer(left, right, width):
    full = jnp.einsum("kim,kjm->kij", left, right, precision=HIGHEST)
    full = full.reshape(full.shape[0], 2, width, 2, width)
    real_part = full[:, 0, :, 0] + full[:, 1, :, 1]
    imag_part = full[:, 1, :, 0] - full[:, 0, :, 1]
    return jnp.stack([real_part, imag_part])


def gelu_pair(values):
    inner = 0.7978845608 * (values + 0.044715 * values * values * values)
    tangent = jnp.tanh(inner)
    output = 0.5 * values * (1.0 + tangent)
    slope = 0.5 * (1.0 + tangent) + 0.5 * values * (1.0 - tangent * tangent) * 0.7978845608 * (
        1.0 + 3.0 * 0.044715 * values * values
    )
    return (output, slope)


def split_parts(stacked, width):
    return jnp.swapaxes(stacked.reshape(stacked.shape[0], 2, width), 0, 1)


def backprop(spectrum, grad_spec, weight_in, bias_in, weight_out):
    width = weight_in.shape[-1]
    forward_in = real_form(weight_in)
    forward_out = real_form(weight_out)
    bias = jnp.concatenate([bias_in[0], bias_in[1]], axis=1)
    before = apply(forward_in, spectrum) + bias[..., None]
    hidden, slope = gelu_pair(before)
    grad_hidden = apply_adjoint(forward_out, grad_spec)
    grad_before = grad_hidden * slope
    grad_modes = apply_adjoint(forward_in, grad_before)
    grad_w_out = complex_outer(grad_spec, hidden, width)
    grad_w_in = complex_outer(grad_before, spectrum, width)
    return (
        grad_modes,
        grad_w_in,
        split_parts(jnp.sum(grad_before, axis=-1), width),
        grad_w_out,
        split_parts(jnp.sum(grad_spec, axis=-1), width),
    )


def to_columns(spectrum, ndev):
    moved = lax.all_to_all(spectrum, "space", split_axis=3, concat_axis=2, tiled=True)
    nblocks, width, rows, _ = moved.shape
    return moved.reshape(nblocks, width, rows, 2, -1)


def sum_over(flat, axis):
    n = lax.axis_size(axis)
    pad = (-flat.shape[0]) % n
    pieces = jnp.pad(flat, (0, pad)).reshape(n, -1)
    got = lax.all_to_all(pieces, axis, split_axis=0, concat_axis=0, tiled=True)
    mine = jnp.sum(got, axis=0)
    spread = jnp.broadcast_to(mine[None], pieces.shape)
    full = lax.all_to_all(spread, axis, split_axis=0, concat_axis=0, tiled=True)
    return full.reshape(-1)[: flat.shape[0]]


def shards(activations, cotangent, kept_modes, weight_in, bias_in, weight_out):
    field = activations[0]
    own_grad = cotangent[0]
    nblocks = field.shape[0]
    width = field.shape[1]
    ndev = lax.axis_size("space")
    received = from_behind(own_grad, "pipe", -1)
    section_index = lax.axis_index("pipe")
    last_section = lax.axis_size("pipe") - 1
    lon_cos, lon_sin = lon_tables(LON, KEEP_LON)
    lat_cos, lat_sin = lat_tables(LAT, KEEP_LAT)
    table = lon_forward_table(lon_cos, lon_sin, ndev)
    col_field = to_columns(lon_forward(field, table), ndev)
    col_field, received = lax.optimization_barrier((col_field, received))
    spectrum = lat_forward(col_field, lat_cos, lat_sin)
    upstream = jnp.where(section_index == last_section, own_grad, received)
    col_grad = to_columns(lon_forward(upstream, table), ndev)
    grad_spec = lat_forward(col_grad, lat_cos, lat_sin)
    share = KEEP_LON // ndev
    signed = jnp.arange(2 * KEEP_LAT, dtype=jnp.int32) - KEEP_LAT
    wavenumber = lax.axis_index("space") * share + jnp.arange(share, dtype=jnp.int32)
    weight = mode_mask(signed, wavenumber, kept_modes[0, 0], kept_modes[0, 1])
    grad_spec = grad_spec * weight
    spectrum = spectrum.reshape(nblocks, 2 * width, -1)
    grad_spec = grad_spec.reshape(nblocks, 2 * width, -1)
    grad_modes, grad_w_in, grad_b_in, grad_w_out, grad_b_out = backprop(
        spectrum, grad_spec, weight_in[0], bias_in[0], weight_out[0]
    )
    grad_modes = grad_modes.reshape(nblocks, 2, width, 2 * KEEP_LAT, share)
    rows = LAT // ndev
    back = lat_inverse_split(grad_modes, lat_cos, lat_sin, ndev).reshape(ndev, -1)
    parts = (grad_w_in, grad_b_in, grad_w_out, grad_b_out)
    flat = jnp.concatenate([p.reshape(-1) for p in parts])
    pad = (-flat.shape[0]) % ndev
    pieces = jnp.pad(flat, (0, pad)).reshape(ndev, -1)
    moved = lax.all_to_all(
        jnp.concatenate([back, pieces], axis=1), "space", split_axis=0, concat_axis=0, tiled=True
    )
    rows_back = moved[:, : back.shape[1]].reshape(ndev, 2, nblocks, width, rows, share)
    mine = jnp.sum(moved[:, back.shape[1]:], axis=0)
    spread = jnp.broadcast_to(mine[None], pieces.shape)
    flat = lax.all_to_all(spread, "space", split_axis=0, concat_axis=0, tiled=True)
    flat = flat.reshape(-1)[: flat.size - pad]
    inverse = lon_inverse_split(rows_back, lon_cos, lon_sin, ndev)
    factor = 1.0 / math.sqrt(2 * KEEP_LAT * KEEP_LON)
    flat = flat * factor
    sums = []
    start = 0
    for p in parts:
        sums.append(flat[start:start + p.size].reshape(p.shape)[None])
        start += p.size
    grad_field = (upstream.astype(jnp.float32) + inverse).astype(jnp.bfloat16)
    return (grad_field[None], *sums)


def solution(mesh):
    return jax.shard_map(
        shards,
        mesh=mesh,
        in_specs=(
            P("pipe", None, None, "space", None),
            P("pipe", None, None, "space", None),
            P("pipe", None),
            P("pipe", None, None, None, None),
            P("pipe", None, None, None),
            P("pipe", None, None, None, None),
        ),
        out_specs=(
            P("pipe", None, None, "space", None),
            P("pipe", None, None, None, None),
            P("pipe", None, None, None),
            P("pipe", None, None, None, None),
            P("pipe", None, None, None),
        ),
        check_vma=False,
    )
```

```python
import math

import jax
import jax.numpy as jnp
from jax import lax
from jax.sharding import PartitionSpec as P

LAT = 256
LON = 512
KEEP_LON = 128
KEEP_LAT = 64


HIGHEST = lax.Precision.HIGH


def from_behind(block, axis, distance):
    devices = range(lax.axis_size(axis))
    route = [(i - distance, i) for i in devices if i - distance in devices]
    return lax.ppermute(block, axis, route)


def lon_tables(length, count):
    column = jnp.arange(length, dtype=jnp.int32)
    number = jnp.arange(count, dtype=jnp.int32)
    phase = column[:, None] * number[None, :] % length
    angle = phase.astype(jnp.float32) * (2.0 * math.pi / length)
    factor = 1.0 / math.sqrt(length)
    return (jnp.cos(angle) * factor, jnp.sin(angle) * factor)


def lat_tables(length, half):
    signed = jnp.arange(2 * half, dtype=jnp.int32) - half
    row_index = jnp.arange(length, dtype=jnp.int32)
    phase = signed[:, None] * row_index[None, :] % length
    angle = phase.astype(jnp.float32) * (2.0 * math.pi / length)
    factor = 1.0 / math.sqrt(length)
    return (jnp.cos(angle) * factor, jnp.sin(angle) * factor)


def lon_forward_table(cos_table, sin_table, ndev):
    share = cos_table.shape[1] // ndev
    cos_g = cos_table.reshape(-1, ndev, 1, share)
    sin_g = -sin_table.reshape(-1, ndev, 1, share)
    return jnp.concatenate([cos_g, sin_g], axis=2).reshape(cos_table.shape[0], -1)


def lon_forward(field, table):
    values = field.astype(jnp.float32)
    return jnp.einsum("ibln,nc->iblc", values, table, precision=HIGHEST)


def lat_forward_table(cos_table, sin_table):
    top = jnp.stack([cos_table, sin_table], axis=1)
    bottom = jnp.stack([-sin_table, cos_table], axis=1)
    return jnp.stack([top, bottom])


def lat_forward(spectrum, table):
    return jnp.einsum("ofpl,iblpj->iobfj", table, spectrum, precision=HIGHEST)


def lat_inverse(spectrum, cos_table, sin_table):
    top = jnp.stack([cos_table, -sin_table])
    bottom = jnp.stack([sin_table, cos_table])
    table = jnp.stack([top, bottom])
    return jnp.einsum("opfl,pibfj->oiblj", table, spectrum, precision=HIGHEST)


def lon_inverse(spectrum, cos_table, sin_table):
    table = jnp.stack([cos_table, -sin_table])
    return jnp.einsum("piblk,pnk->ibln", spectrum, table, precision=HIGHEST)


def lat_inverse_table(cos_table, sin_table, ndev):
    top = jnp.stack([cos_table, -sin_table])
    bottom = jnp.stack([sin_table, cos_table])
    table = jnp.stack([top, bottom])
    return table.reshape(table.shape[:3] + (ndev, -1))


def lat_inverse_split(spectrum, table):
    return jnp.einsum("opfdr,ipbfj->doibrj", table, spectrum, precision=HIGHEST)


def lon_inverse_table(cos_table, sin_table, ndev):
    table = jnp.stack([cos_table, -sin_table])
    return table.reshape(table.shape[:2] + (ndev, -1))


def lon_inverse_split(spectrum, table):
    return jnp.einsum("dpiblj,pndj->ibln", spectrum, table, precision=HIGHEST)


def mode_mask(signed, wavenumber, keep_lon, keep_lat):
    lat_kept = (signed >= -keep_lat) & (signed < keep_lat)
    lon_kept = wavenumber < keep_lon
    factor = jnp.where(wavenumber == 0, 1.0, 2.0).astype(jnp.float32)
    return (lat_kept[:, None] & lon_kept[None, :]).astype(jnp.float32) * factor[None, :]


def real_form(weights):
    real_part, imag_part = weights[0], weights[1]
    top = jnp.concatenate([real_part, -imag_part], axis=2)
    bottom = jnp.concatenate([imag_part, real_part], axis=2)
    return jnp.concatenate([top, bottom], axis=1)


def apply(weights, values):
    return jnp.einsum("kij,kjm->kim", weights, values, precision=HIGHEST)


def apply_adjoint(weights, values):
    return jnp.einsum("kji,kjm->kim", weights, values, precision=HIGHEST)


def complex_outer(left, right, width):
    full = jnp.einsum("kim,kjm->kij", left, right, precision=HIGHEST)
    full = full.reshape(full.shape[0], 2, width, 2, width)
    real_part = full[:, 0, :, 0] + full[:, 1, :, 1]
    imag_part = full[:, 1, :, 0] - full[:, 0, :, 1]
    return jnp.stack([real_part, imag_part])


def gelu_pair(values):
    inner = 0.7978845608 * (values + 0.044715 * values * values * values)
    tangent = jnp.tanh(inner)
    output = 0.5 * values * (1.0 + tangent)
    slope = 0.5 * (1.0 + tangent) + 0.5 * values * (1.0 - tangent * tangent) * 0.7978845608 * (
        1.0 + 3.0 * 0.044715 * values * values
    )
    return (output, slope)


def split_parts(stacked, width):
    return jnp.swapaxes(stacked.reshape(stacked.shape[0], 2, width), 0, 1)


def backprop(spectrum, grad_spec, weight_in, bias_in, weight_out):
    width = weight_in.shape[-1]
    forward_in = real_form(weight_in)
    forward_out = real_form(weight_out)
    bias = jnp.concatenate([bias_in[0], bias_in[1]], axis=1)
    before = apply(forward_in, spectrum) + bias[..., None]
    hidden, slope = gelu_pair(before)
    grad_hidden = apply_adjoint(forward_out, grad_spec)
    grad_before = grad_hidden * slope
    grad_modes = apply_adjoint(forward_in, grad_before)
    grad_w_out = complex_outer(grad_spec, hidden, width)
    grad_w_in = complex_outer(grad_before, spectrum, width)
    return (
        grad_modes,
        grad_w_in,
        split_parts(jnp.sum(grad_before, axis=-1), width),
        grad_w_out,
        split_parts(jnp.sum(grad_spec, axis=-1), width),
    )


def to_columns(spectrum, ndev):
    moved = lax.all_to_all(spectrum, "space", split_axis=3, concat_axis=2, tiled=True)
    nblocks, width, rows, _ = moved.shape
    return moved.reshape(nblocks, width, rows, 2, -1)


def sum_over(flat, axis):
    n = lax.axis_size(axis)
    pad = (-flat.shape[0]) % n
    pieces = jnp.pad(flat, (0, pad)).reshape(n, -1)
    got = lax.all_to_all(pieces, axis, split_axis=0, concat_axis=0, tiled=True)
    mine = jnp.sum(got, axis=0)
    spread = jnp.broadcast_to(mine[None], pieces.shape)
    full = lax.all_to_all(spread, axis, split_axis=0, concat_axis=0, tiled=True)
    return full.reshape(-1)[: flat.shape[0]]


def shards(activations, cotangent, kept_modes, weight_in, bias_in, weight_out):
    field = activations[0]
    own_grad = cotangent[0]
    nblocks = field.shape[0]
    width = field.shape[1]
    ndev = lax.axis_size("space")
    received = from_behind(own_grad, "pipe", -1)
    section_index = lax.axis_index("pipe")
    last_section = lax.axis_size("pipe") - 1
    lon_cos, lon_sin = lon_tables(LON, KEEP_LON)
    lat_cos, lat_sin = lat_tables(LAT, KEEP_LAT)
    table = lon_forward_table(lon_cos, lon_sin, ndev)
    share = KEEP_LON // ndev
    signed = jnp.arange(2 * KEEP_LAT, dtype=jnp.int32) - KEEP_LAT
    wavenumber = lax.axis_index("space") * share + jnp.arange(share, dtype=jnp.int32)
    weight = mode_mask(signed, wavenumber, kept_modes[0, 0], kept_modes[0, 1])
    tables = (
        lat_forward_table(lat_cos, lat_sin),
        lat_inverse_table(lat_cos, lat_sin, ndev),
        lon_inverse_table(lon_cos, lon_sin, ndev),
        weight,
    )
    col_field = to_columns(lon_forward(field, table), ndev)
    col_field, received, tables = lax.optimization_barrier((col_field, received, tables))
    lat_table, lat_back_table, lon_back_table, weight = tables
    spectrum = lat_forward(col_field, lat_table)
    upstream = jnp.where(section_index == last_section, own_grad, received)
    col_grad = to_columns(lon_forward(upstream, table), ndev)
    grad_spec = lat_forward(col_grad, lat_table)
    grad_spec = grad_spec * weight
    spectrum = spectrum.reshape(nblocks, 2 * width, -1)
    grad_spec = grad_spec.reshape(nblocks, 2 * width, -1)
    grad_modes, grad_w_in, grad_b_in, grad_w_out, grad_b_out = backprop(
        spectrum, grad_spec, weight_in[0], bias_in[0], weight_out[0]
    )
    grad_modes = grad_modes.reshape(nblocks, 2, width, 2 * KEEP_LAT, share)
    rows = LAT // ndev
    back = lat_inverse_split(grad_modes, lat_back_table).reshape(ndev, -1)
    parts = (grad_w_in, grad_b_in, grad_w_out, grad_b_out)
    flat = jnp.concatenate([p.reshape(-1) for p in parts])
    pad = (-flat.shape[0]) % ndev
    pieces = jnp.pad(flat, (0, pad)).reshape(ndev, -1)
    moved = lax.all_to_all(
        jnp.concatenate([back, pieces], axis=1), "space", split_axis=0, concat_axis=0, tiled=True
    )
    rows_back = moved[:, : back.shape[1]].reshape(ndev, 2, nblocks, width, rows, share)
    mine = jnp.sum(moved[:, back.shape[1]:], axis=0)
    spread = jnp.broadcast_to(mine[None], pieces.shape)
    flat = lax.all_to_all(spread, "space", split_axis=0, concat_axis=0, tiled=True)
    flat = flat.reshape(-1)[: flat.size - pad]
    inverse = lon_inverse_split(rows_back, lon_back_table)
    factor = 1.0 / math.sqrt(2 * KEEP_LAT * KEEP_LON)
    flat = flat * factor
    sums = []
    start = 0
    for p in parts:
        sums.append(flat[start:start + p.size].reshape(p.shape)[None])
        start += p.size
    grad_field = (upstream.astype(jnp.float32) + inverse).astype(jnp.bfloat16)
    return (grad_field[None], *sums)


def solution(mesh):
    return jax.shard_map(
        shards,
        mesh=mesh,
        in_specs=(
            P("pipe", None, None, "space", None),
            P("pipe", None, None, "space", None),
            P("pipe", None),
            P("pipe", None, None, None, None),
            P("pipe", None, None, None),
            P("pipe", None, None, None, None),
        ),
        out_specs=(
            P("pipe", None, None, "space", None),
            P("pipe", None, None, None, None),
            P("pipe", None, None, None),
            P("pipe", None, None, None, None),
            P("pipe", None, None, None),
        ),
        check_vma=False,
    )
```

```python
import math

import jax
import jax.numpy as jnp
from jax import lax
from jax.sharding import PartitionSpec as P

LAT = 256
LON = 512
KEEP_LON = 128
KEEP_LAT = 64


HIGHEST = lax.Precision.HIGH


def from_behind(block, axis, distance):
    devices = range(lax.axis_size(axis))
    route = [(i - distance, i) for i in devices if i - distance in devices]
    return lax.ppermute(block, axis, route)


def lon_tables(length, count):
    column = jnp.arange(length, dtype=jnp.int32)
    number = jnp.arange(count, dtype=jnp.int32)
    phase = column[:, None] * number[None, :] % length
    angle = phase.astype(jnp.float32) * (2.0 * math.pi / length)
    factor = 1.0 / math.sqrt(length)
    return (jnp.cos(angle) * factor, jnp.sin(angle) * factor)


def lat_tables(length, half):
    signed = jnp.arange(2 * half, dtype=jnp.int32) - half
    row_index = jnp.arange(length, dtype=jnp.int32)
    phase = signed[:, None] * row_index[None, :] % length
    angle = phase.astype(jnp.float32) * (2.0 * math.pi / length)
    factor = 1.0 / math.sqrt(length)
    return (jnp.cos(angle) * factor, jnp.sin(angle) * factor)


def lon_forward_table(cos_table, sin_table, ndev):
    share = cos_table.shape[1] // ndev
    cos_g = cos_table.reshape(-1, ndev, 1, share)
    sin_g = -sin_table.reshape(-1, ndev, 1, share)
    return jnp.concatenate([cos_g, sin_g], axis=2).reshape(cos_table.shape[0], -1)


def lon_forward(field, table):
    values = field.astype(jnp.float32)
    return jnp.einsum("ibln,nc->iblc", values, table, precision=HIGHEST)


def lat_forward(spectrum, cos_table, sin_table):
    top = jnp.stack([cos_table, sin_table], axis=1)
    bottom = jnp.stack([-sin_table, cos_table], axis=1)
    table = jnp.stack([top, bottom])
    return jnp.einsum("ofpl,iblpj->iobfj", table, spectrum, precision=HIGHEST)


def lat_inverse(spectrum, cos_table, sin_table):
    top = jnp.stack([cos_table, -sin_table])
    bottom = jnp.stack([sin_table, cos_table])
    table = jnp.stack([top, bottom])
    return jnp.einsum("opfl,pibfj->oiblj", table, spectrum, precision=HIGHEST)


def lon_inverse(spectrum, cos_table, sin_table):
    table = jnp.stack([cos_table, -sin_table])
    return jnp.einsum("piblk,pnk->ibln", spectrum, table, precision=HIGHEST)


def lat_inverse_split(spectrum, cos_table, sin_table, ndev):
    top = jnp.stack([cos_table, -sin_table])
    bottom = jnp.stack([sin_table, cos_table])
    table = jnp.stack([top, bottom])
    table = table.reshape(table.shape[:3] + (ndev, -1))
    return jnp.einsum("opfdr,ipbfj->doibrj", table, spectrum, precision=HIGHEST)


def lon_inverse_split(spectrum, cos_table, sin_table, ndev):
    table = jnp.stack([cos_table, -sin_table])
    table = table.reshape(table.shape[:2] + (ndev, -1))
    return jnp.einsum("dpiblj,pndj->ibln", spectrum, table, precision=HIGHEST)


def mode_mask(signed, wavenumber, keep_lon, keep_lat):
    lat_kept = (signed >= -keep_lat) & (signed < keep_lat)
    lon_kept = wavenumber < keep_lon
    factor = jnp.where(wavenumber == 0, 1.0, 2.0).astype(jnp.float32)
    return (lat_kept[:, None] & lon_kept[None, :]).astype(jnp.float32) * factor[None, :]


def real_form(weights):
    real_part, imag_part = weights[0], weights[1]
    top = jnp.concatenate([real_part, -imag_part], axis=2)
    bottom = jnp.concatenate([imag_part, real_part], axis=2)
    return jnp.concatenate([top, bottom], axis=1)


def apply(weights, values):
    return jnp.einsum("kij,kjm->kim", weights, values, precision=HIGHEST)


def apply_adjoint(weights, values):
    return jnp.einsum("kji,kjm->kim", weights, values, precision=HIGHEST)


def complex_outer(left, right, width):
    full = jnp.einsum("kim,kjm->kij", left, right, precision=HIGHEST)
    full = full.reshape(full.shape[0], 2, width, 2, width)
    real_part = full[:, 0, :, 0] + full[:, 1, :, 1]
    imag_part = full[:, 1, :, 0] - full[:, 0, :, 1]
    return jnp.stack([real_part, imag_part])


def gelu_pair(values):
    inner = 0.7978845608 * (values + 0.044715 * values * values * values)
    tangent = jnp.tanh(inner)
    output = 0.5 * values * (1.0 + tangent)
    slope = 0.5 * (1.0 + tangent) + 0.5 * values * (1.0 - tangent * tangent) * 0.7978845608 * (
        1.0 + 3.0 * 0.044715 * values * values
    )
    return (output, slope)


def split_parts(stacked, width):
    return jnp.swapaxes(stacked.reshape(stacked.shape[0], 2, width), 0, 1)


def backprop(spectrum, grad_spec, weight_in, bias_in, weight_out):
    width = weight_in.shape[-1]
    forward_in = real_form(weight_in)
    forward_out = real_form(weight_out)
    bias = jnp.concatenate([bias_in[0], bias_in[1]], axis=1)
    before = apply(forward_in, spectrum) + bias[..., None]
    hidden, slope = gelu_pair(before)
    grad_hidden = apply_adjoint(forward_out, grad_spec)
    grad_before = grad_hidden * slope
    grad_modes = apply_adjoint(forward_in, grad_before)
    grad_w_out = complex_outer(grad_spec, hidden, width)
    grad_w_in = complex_outer(grad_before, spectrum, width)
    return (
        grad_modes,
        grad_w_in,
        split_parts(jnp.sum(grad_before, axis=-1), width),
        grad_w_out,
        split_parts(jnp.sum(grad_spec, axis=-1), width),
    )


def to_columns(spectrum, ndev):
    moved = lax.all_to_all(spectrum, "space", split_axis=3, concat_axis=2, tiled=True)
    nblocks, width, rows, _ = moved.shape
    return moved.reshape(nblocks, width, rows, 2, -1)


def sum_over(flat, axis):
    n = lax.axis_size(axis)
    pad = (-flat.shape[0]) % n
    pieces = jnp.pad(flat, (0, pad)).reshape(n, -1)
    got = lax.all_to_all(pieces, axis, split_axis=0, concat_axis=0, tiled=True)
    mine = jnp.sum(got, axis=0)
    spread = jnp.broadcast_to(mine[None], pieces.shape)
    full = lax.all_to_all(spread, axis, split_axis=0, concat_axis=0, tiled=True)
    return full.reshape(-1)[: flat.shape[0]]


def shards(activations, cotangent, kept_modes, weight_in, bias_in, weight_out):
    field = activations[0]
    own_grad = cotangent[0]
    nblocks = field.shape[0]
    width = field.shape[1]
    ndev = lax.axis_size("space")
    received = from_behind(own_grad, "pipe", -1)
    section_index = lax.axis_index("pipe")
    last_section = lax.axis_size("pipe") - 1
    lon_cos, lon_sin = lon_tables(LON, KEEP_LON)
    lat_cos, lat_sin = lat_tables(LAT, KEEP_LAT)
    table = lon_forward_table(lon_cos, lon_sin, ndev)
    col_field = to_columns(lon_forward(field, table), ndev)
    upstream = jnp.where(section_index == last_section, own_grad, received)
    col_field, lon_grad = lax.optimization_barrier((col_field, lon_forward(upstream, table)))
    spectrum = lat_forward(col_field, lat_cos, lat_sin)
    col_grad = to_columns(lon_grad, ndev)
    grad_spec = lat_forward(col_grad, lat_cos, lat_sin)
    share = KEEP_LON // ndev
    signed = jnp.arange(2 * KEEP_LAT, dtype=jnp.int32) - KEEP_LAT
    wavenumber = lax.axis_index("space") * share + jnp.arange(share, dtype=jnp.int32)
    weight = mode_mask(signed, wavenumber, kept_modes[0, 0], kept_modes[0, 1])
    grad_spec = grad_spec * weight
    spectrum = spectrum.reshape(nblocks, 2 * width, -1)
    grad_spec = grad_spec.reshape(nblocks, 2 * width, -1)
    grad_modes, grad_w_in, grad_b_in, grad_w_out, grad_b_out = backprop(
        spectrum, grad_spec, weight_in[0], bias_in[0], weight_out[0]
    )
    grad_modes = grad_modes.reshape(nblocks, 2, width, 2 * KEEP_LAT, share)
    rows = LAT // ndev
    back = lat_inverse_split(grad_modes, lat_cos, lat_sin, ndev).reshape(ndev, -1)
    parts = (grad_w_in, grad_b_in, grad_w_out, grad_b_out)
    flat = jnp.concatenate([p.reshape(-1) for p in parts])
    pad = (-flat.shape[0]) % ndev
    pieces = jnp.pad(flat, (0, pad)).reshape(ndev, -1)
    moved = lax.all_to_all(
        jnp.concatenate([back, pieces], axis=1), "space", split_axis=0, concat_axis=0, tiled=True
    )
    rows_back = moved[:, : back.shape[1]].reshape(ndev, 2, nblocks, width, rows, share)
    mine = jnp.sum(moved[:, back.shape[1]:], axis=0)
    spread = jnp.broadcast_to(mine[None], pieces.shape)
    flat = lax.all_to_all(spread, "space", split_axis=0, concat_axis=0, tiled=True)
    flat = flat.reshape(-1)[: flat.size - pad]
    inverse = lon_inverse_split(rows_back, lon_cos, lon_sin, ndev)
    factor = 1.0 / math.sqrt(2 * KEEP_LAT * KEEP_LON)
    flat = flat * factor
    sums = []
    start = 0
    for p in parts:
        sums.append(flat[start:start + p.size].reshape(p.shape)[None])
        start += p.size
    grad_field = (upstream.astype(jnp.float32) + inverse).astype(jnp.bfloat16)
    return (grad_field[None], *sums)


def solution(mesh):
    return jax.shard_map(
        shards,
        mesh=mesh,
        in_specs=(
            P("pipe", None, None, "space", None),
            P("pipe", None, None, "space", None),
            P("pipe", None),
            P("pipe", None, None, None, None),
            P("pipe", None, None, None),
            P("pipe", None, None, None, None),
        ),
        out_specs=(
            P("pipe", None, None, "space", None),
            P("pipe", None, None, None, None),
            P("pipe", None, None, None),
            P("pipe", None, None, None, None),
            P("pipe", None, None, None),
        ),
        check_vma=False,
    )
```

```python
import math

import jax
import jax.numpy as jnp
from jax import lax
from jax.sharding import PartitionSpec as P

LAT = 256
LON = 512
KEEP_LON = 128
KEEP_LAT = 64


HIGHEST = lax.Precision.HIGH


def from_behind(block, axis, distance):
    devices = range(lax.axis_size(axis))
    route = [(i - distance, i) for i in devices if i - distance in devices]
    return lax.ppermute(block, axis, route)


def lon_tables(length, count):
    column = jnp.arange(length, dtype=jnp.int32)
    number = jnp.arange(count, dtype=jnp.int32)
    phase = column[:, None] * number[None, :] % length
    angle = phase.astype(jnp.float32) * (2.0 * math.pi / length)
    factor = 1.0 / math.sqrt(length)
    return (jnp.cos(angle) * factor, jnp.sin(angle) * factor)


def lat_tables(length, half):
    signed = jnp.arange(2 * half, dtype=jnp.int32) - half
    row_index = jnp.arange(length, dtype=jnp.int32)
    phase = signed[:, None] * row_index[None, :] % length
    angle = phase.astype(jnp.float32) * (2.0 * math.pi / length)
    factor = 1.0 / math.sqrt(length)
    return (jnp.cos(angle) * factor, jnp.sin(angle) * factor)


def lon_forward_table(cos_table, sin_table, ndev):
    share = cos_table.shape[1] // ndev
    cos_g = cos_table.reshape(-1, ndev, 1, share)
    sin_g = -sin_table.reshape(-1, ndev, 1, share)
    return jnp.concatenate([cos_g, sin_g], axis=2).reshape(cos_table.shape[0], -1)


def lon_forward(field, table):
    values = field.astype(jnp.float32)
    return jnp.einsum("ibln,nc->iblc", values, table, precision=HIGHEST)


def lat_forward(spectrum, cos_table, sin_table):
    top = jnp.stack([cos_table, sin_table], axis=1)
    bottom = jnp.stack([-sin_table, cos_table], axis=1)
    table = jnp.stack([top, bottom])
    return jnp.einsum("ofpl,iblpj->iobfj", table, spectrum, precision=HIGHEST)


def lat_inverse(spectrum, cos_table, sin_table):
    top = jnp.stack([cos_table, -sin_table])
    bottom = jnp.stack([sin_table, cos_table])
    table = jnp.stack([top, bottom])
    return jnp.einsum("opfl,pibfj->oiblj", table, spectrum, precision=HIGHEST)


def lon_inverse(spectrum, cos_table, sin_table):
    table = jnp.stack([cos_table, -sin_table])
    return jnp.einsum("piblk,pnk->ibln", spectrum, table, precision=HIGHEST)


def lat_inverse_split(spectrum, cos_table, sin_table, ndev):
    top = jnp.stack([cos_table, -sin_table])
    bottom = jnp.stack([sin_table, cos_table])
    table = jnp.stack([top, bottom])
    table = table.reshape(table.shape[:3] + (ndev, -1))
    return jnp.einsum("opfdr,ipbfj->doibrj", table, spectrum, precision=HIGHEST)


def lon_inverse_split(spectrum, cos_table, sin_table, ndev):
    table = jnp.stack([cos_table, -sin_table])
    table = table.reshape(table.shape[:2] + (ndev, -1))
    return jnp.einsum("dpiblj,pndj->ibln", spectrum, table, precision=HIGHEST)


def mode_mask(signed, wavenumber, keep_lon, keep_lat):
    lat_kept = (signed >= -keep_lat) & (signed < keep_lat)
    lon_kept = wavenumber < keep_lon
    factor = jnp.where(wavenumber == 0, 1.0, 2.0).astype(jnp.float32)
    return (lat_kept[:, None] & lon_kept[None, :]).astype(jnp.float32) * factor[None, :]


def real_form(weights):
    real_part, imag_part = weights[0], weights[1]
    top = jnp.concatenate([real_part, -imag_part], axis=2)
    bottom = jnp.concatenate([imag_part, real_part], axis=2)
    return jnp.concatenate([top, bottom], axis=1)


def apply(weights, values):
    return jnp.einsum("kij,kjm->kim", weights, values, precision=HIGHEST)


def apply_adjoint(weights, values):
    return jnp.einsum("kji,kjm->kim", weights, values, precision=HIGHEST)


def complex_outer(left, right, width):
    full = jnp.einsum("kim,kjm->kij", left, right, precision=HIGHEST)
    full = full.reshape(full.shape[0], 2, width, 2, width)
    real_part = full[:, 0, :, 0] + full[:, 1, :, 1]
    imag_part = full[:, 1, :, 0] - full[:, 0, :, 1]
    return jnp.stack([real_part, imag_part])


def gelu_pair(values):
    inner = 0.7978845608 * (values + 0.044715 * values * values * values)
    tangent = jnp.tanh(inner)
    output = 0.5 * values * (1.0 + tangent)
    slope = 0.5 * (1.0 + tangent) + 0.5 * values * (1.0 - tangent * tangent) * 0.7978845608 * (
        1.0 + 3.0 * 0.044715 * values * values
    )
    return (output, slope)


def split_parts(stacked, width):
    return jnp.swapaxes(stacked.reshape(stacked.shape[0], 2, width), 0, 1)


def backprop(spectrum, grad_spec, weight_in, bias_in, weight_out):
    width = weight_in.shape[-1]
    forward_in = real_form(weight_in)
    forward_out = real_form(weight_out)
    bias = jnp.concatenate([bias_in[0], bias_in[1]], axis=1)
    before = apply(forward_in, spectrum) + bias[..., None]
    hidden, slope = gelu_pair(before)
    grad_hidden = apply_adjoint(forward_out, grad_spec)
    grad_before = grad_hidden * slope
    grad_modes = apply_adjoint(forward_in, grad_before)
    grad_w_out = complex_outer(grad_spec, hidden, width)
    grad_w_in = complex_outer(grad_before, spectrum, width)
    return (
        grad_modes,
        grad_w_in,
        split_parts(jnp.sum(grad_before, axis=-1), width),
        grad_w_out,
        split_parts(jnp.sum(grad_spec, axis=-1), width),
    )


def to_columns(spectrum, ndev):
    moved = lax.all_to_all(spectrum, "space", split_axis=3, concat_axis=2, tiled=True)
    nblocks, width, rows, _ = moved.shape
    return moved.reshape(nblocks, width, rows, 2, -1)


def sum_over(flat, axis):
    n = lax.axis_size(axis)
    pad = (-flat.shape[0]) % n
    pieces = jnp.pad(flat, (0, pad)).reshape(n, -1)
    got = lax.all_to_all(pieces, axis, split_axis=0, concat_axis=0, tiled=True)
    mine = jnp.sum(got, axis=0)
    spread = jnp.broadcast_to(mine[None], pieces.shape)
    full = lax.all_to_all(spread, axis, split_axis=0, concat_axis=0, tiled=True)
    return full.reshape(-1)[: flat.shape[0]]


def shards(activations, cotangent, kept_modes, weight_in, bias_in, weight_out):
    field = activations[0]
    own_grad = cotangent[0]
    nblocks = field.shape[0]
    width = field.shape[1]
    ndev = lax.axis_size("space")
    received = from_behind(own_grad, "pipe", -1)
    section_index = lax.axis_index("pipe")
    last_section = lax.axis_size("pipe") - 1
    lon_cos, lon_sin = lon_tables(LON, KEEP_LON)
    lat_cos, lat_sin = lat_tables(LAT, KEEP_LAT)
    table = lon_forward_table(lon_cos, lon_sin, ndev)
    own_lon = lon_forward(own_grad, table)
    received_lon = from_behind(own_lon, "pipe", -1)
    col_field = to_columns(lon_forward(field, table), ndev)
    upstream_lon = jnp.where(section_index == last_section, own_lon, received_lon)
    col_field, upstream_lon = lax.optimization_barrier((col_field, upstream_lon))
    spectrum = lat_forward(col_field, lat_cos, lat_sin)
    col_grad = to_columns(upstream_lon, ndev)
    grad_spec = lat_forward(col_grad, lat_cos, lat_sin)
    share = KEEP_LON // ndev
    signed = jnp.arange(2 * KEEP_LAT, dtype=jnp.int32) - KEEP_LAT
    wavenumber = lax.axis_index("space") * share + jnp.arange(share, dtype=jnp.int32)
    weight = mode_mask(signed, wavenumber, kept_modes[0, 0], kept_modes[0, 1])
    grad_spec = grad_spec * weight
    spectrum = spectrum.reshape(nblocks, 2 * width, -1)
    grad_spec = grad_spec.reshape(nblocks, 2 * width, -1)
    grad_modes, grad_w_in, grad_b_in, grad_w_out, grad_b_out = backprop(
        spectrum, grad_spec, weight_in[0], bias_in[0], weight_out[0]
    )
    grad_modes = grad_modes.reshape(nblocks, 2, width, 2 * KEEP_LAT, share)
    rows = LAT // ndev
    back = lat_inverse_split(grad_modes, lat_cos, lat_sin, ndev).reshape(ndev, -1)
    parts = (grad_w_in, grad_b_in, grad_w_out, grad_b_out)
    flat = jnp.concatenate([p.reshape(-1) for p in parts])
    pad = (-flat.shape[0]) % ndev
    pieces = jnp.pad(flat, (0, pad)).reshape(ndev, -1)
    joined, received = lax.optimization_barrier((jnp.concatenate([back, pieces], axis=1), received))
    moved = lax.all_to_all(joined, "space", split_axis=0, concat_axis=0, tiled=True)
    rows_back = moved[:, : back.shape[1]].reshape(ndev, 2, nblocks, width, rows, share)
    mine = jnp.sum(moved[:, back.shape[1]:], axis=0)
    spread = jnp.broadcast_to(mine[None], pieces.shape)
    flat = lax.all_to_all(spread, "space", split_axis=0, concat_axis=0, tiled=True)
    flat = flat.reshape(-1)[: flat.size - pad]
    inverse = lon_inverse_split(rows_back, lon_cos, lon_sin, ndev)
    factor = 1.0 / math.sqrt(2 * KEEP_LAT * KEEP_LON)
    flat = flat * factor
    sums = []
    start = 0
    for p in parts:
        sums.append(flat[start:start + p.size].reshape(p.shape)[None])
        start += p.size
    upstream = jnp.where(section_index == last_section, own_grad, received)
    grad_field = (upstream.astype(jnp.float32) + inverse).astype(jnp.bfloat16)
    return (grad_field[None], *sums)


def solution(mesh):
    return jax.shard_map(
        shards,
        mesh=mesh,
        in_specs=(
            P("pipe", None, None, "space", None),
            P("pipe", None, None, "space", None),
            P("pipe", None),
            P("pipe", None, None, None, None),
            P("pipe", None, None, None),
            P("pipe", None, None, None, None),
        ),
        out_specs=(
            P("pipe", None, None, "space", None),
            P("pipe", None, None, None, None),
            P("pipe", None, None, None),
            P("pipe", None, None, None, None),
            P("pipe", None, None, None),
        ),
        check_vma=False,
    )
```

```python
import math

import jax
import jax.numpy as jnp
from jax import lax
from jax.sharding import PartitionSpec as P

LAT = 256
LON = 512
KEEP_LON = 128
KEEP_LAT = 64


HIGHEST = lax.Precision.HIGH


def from_behind(block, axis, distance):
    devices = range(lax.axis_size(axis))
    route = [(i - distance, i) for i in devices if i - distance in devices]
    return lax.ppermute(block, axis, route)


def lon_tables(length, count):
    column = jnp.arange(length, dtype=jnp.int32)
    number = jnp.arange(count, dtype=jnp.int32)
    phase = column[:, None] * number[None, :] % length
    angle = phase.astype(jnp.float32) * (2.0 * math.pi / length)
    factor = 1.0 / math.sqrt(length)
    return (jnp.cos(angle) * factor, jnp.sin(angle) * factor)


def lat_tables(length, half):
    signed = jnp.arange(2 * half, dtype=jnp.int32) - half
    row_index = jnp.arange(length, dtype=jnp.int32)
    phase = signed[:, None] * row_index[None, :] % length
    angle = phase.astype(jnp.float32) * (2.0 * math.pi / length)
    factor = 1.0 / math.sqrt(length)
    return (jnp.cos(angle) * factor, jnp.sin(angle) * factor)


def lon_forward_table(cos_table, sin_table, ndev):
    share = cos_table.shape[1] // ndev
    cos_g = cos_table.reshape(-1, ndev, 1, share)
    sin_g = -sin_table.reshape(-1, ndev, 1, share)
    return jnp.concatenate([cos_g, sin_g], axis=2).reshape(cos_table.shape[0], -1)


def lon_forward(field, table):
    values = field.astype(jnp.float32)
    return jnp.einsum("ibln,nc->iblc", values, table, precision=HIGHEST)


def lat_forward(spectrum, cos_table, sin_table):
    top = jnp.stack([cos_table, sin_table], axis=1)
    bottom = jnp.stack([-sin_table, cos_table], axis=1)
    table = jnp.stack([top, bottom])
    return jnp.einsum("ofpl,iblpj->iobfj", table, spectrum, precision=HIGHEST)


def lat_inverse(spectrum, cos_table, sin_table):
    top = jnp.stack([cos_table, -sin_table])
    bottom = jnp.stack([sin_table, cos_table])
    table = jnp.stack([top, bottom])
    return jnp.einsum("opfl,pibfj->oiblj", table, spectrum, precision=HIGHEST)


def lon_inverse(spectrum, cos_table, sin_table):
    table = jnp.stack([cos_table, -sin_table])
    return jnp.einsum("piblk,pnk->ibln", spectrum, table, precision=HIGHEST)


def lat_inverse_split(spectrum, cos_table, sin_table, ndev):
    top = jnp.stack([cos_table, -sin_table])
    bottom = jnp.stack([sin_table, cos_table])
    table = jnp.stack([top, bottom])
    table = table.reshape(table.shape[:3] + (ndev, -1))
    return jnp.einsum("opfdr,ipbfj->doibrj", table, spectrum, precision=HIGHEST)


def lon_inverse_split(spectrum, cos_table, sin_table, ndev):
    table = jnp.stack([cos_table, -sin_table])
    table = table.reshape(table.shape[:2] + (ndev, -1))
    return jnp.einsum("dpiblj,pndj->ibln", spectrum, table, precision=HIGHEST)


def mode_mask(signed, wavenumber, keep_lon, keep_lat):
    lat_kept = (signed >= -keep_lat) & (signed < keep_lat)
    lon_kept = wavenumber < keep_lon
    factor = jnp.where(wavenumber == 0, 1.0, 2.0).astype(jnp.float32)
    return (lat_kept[:, None] & lon_kept[None, :]).astype(jnp.float32) * factor[None, :]


def real_form(weights):
    real_part, imag_part = weights[0], weights[1]
    top = jnp.concatenate([real_part, -imag_part], axis=2)
    bottom = jnp.concatenate([imag_part, real_part], axis=2)
    return jnp.concatenate([top, bottom], axis=1)


def apply(weights, values):
    return jnp.einsum("kij,kjm->kim", weights, values, precision=HIGHEST)


def apply_adjoint(weights, values):
    return jnp.einsum("kji,kjm->kim", weights, values, precision=HIGHEST)


def complex_outer(left, right, width):
    full = jnp.einsum("kim,kjm->kij", left, right, precision=HIGHEST)
    full = full.reshape(full.shape[0], 2, width, 2, width)
    real_part = full[:, 0, :, 0] + full[:, 1, :, 1]
    imag_part = full[:, 1, :, 0] - full[:, 0, :, 1]
    return jnp.stack([real_part, imag_part])


def gelu_pair(values):
    inner = 0.7978845608 * (values + 0.044715 * values * values * values)
    tangent = jnp.tanh(inner)
    output = 0.5 * values * (1.0 + tangent)
    slope = 0.5 * (1.0 + tangent) + 0.5 * values * (1.0 - tangent * tangent) * 0.7978845608 * (
        1.0 + 3.0 * 0.044715 * values * values
    )
    return (output, slope)


def split_parts(stacked, width):
    return jnp.swapaxes(stacked.reshape(stacked.shape[0], 2, width), 0, 1)


def backprop(spectrum, grad_spec, weight_in, bias_in, weight_out):
    width = weight_in.shape[-1]
    forward_in = real_form(weight_in)
    forward_out = real_form(weight_out)
    bias = jnp.concatenate([bias_in[0], bias_in[1]], axis=1)
    before = apply(forward_in, spectrum) + bias[..., None]
    hidden, slope = gelu_pair(before)
    grad_hidden = apply_adjoint(forward_out, grad_spec)
    grad_before = grad_hidden * slope
    grad_modes = apply_adjoint(forward_in, grad_before)
    grad_w_out = complex_outer(grad_spec, hidden, width)
    grad_w_in = complex_outer(grad_before, spectrum, width)
    return (
        grad_modes,
        grad_w_in,
        split_parts(jnp.sum(grad_before, axis=-1), width),
        grad_w_out,
        split_parts(jnp.sum(grad_spec, axis=-1), width),
    )


def to_columns(spectrum, ndev):
    moved = lax.all_to_all(spectrum, "space", split_axis=3, concat_axis=2, tiled=True)
    nblocks, width, rows, _ = moved.shape
    return moved.reshape(nblocks, width, rows, 2, -1)


def sum_over(flat, axis):
    n = lax.axis_size(axis)
    pad = (-flat.shape[0]) % n
    pieces = jnp.pad(flat, (0, pad)).reshape(n, -1)
    got = lax.all_to_all(pieces, axis, split_axis=0, concat_axis=0, tiled=True)
    mine = jnp.sum(got, axis=0)
    spread = jnp.broadcast_to(mine[None], pieces.shape)
    full = lax.all_to_all(spread, axis, split_axis=0, concat_axis=0, tiled=True)
    return full.reshape(-1)[: flat.shape[0]]


def shards(activations, cotangent, kept_modes, weight_in, bias_in, weight_out):
    field = activations[0]
    own_grad = cotangent[0]
    nblocks = field.shape[0]
    width = field.shape[1]
    ndev = lax.axis_size("space")
    section_index = lax.axis_index("pipe")
    last_section = lax.axis_size("pipe") - 1
    lon_cos, lon_sin = lon_tables(LON, KEEP_LON)
    lat_cos, lat_sin = lat_tables(LAT, KEEP_LAT)
    table = lon_forward_table(lon_cos, lon_sin, ndev)
    field_lon, own_grad = lax.optimization_barrier((lon_forward(field, table), own_grad))
    col_field = to_columns(field_lon, ndev)
    own_lon = lon_forward(own_grad, table)
    received_lon = from_behind(own_lon, "pipe", -1)
    received = from_behind(own_grad, "pipe", -1)
    upstream_lon = jnp.where(section_index == last_section, own_lon, received_lon)
    col_field, upstream_lon = lax.optimization_barrier((col_field, upstream_lon))
    spectrum = lat_forward(col_field, lat_cos, lat_sin)
    col_grad = to_columns(upstream_lon, ndev)
    grad_spec = lat_forward(col_grad, lat_cos, lat_sin)
    share = KEEP_LON // ndev
    signed = jnp.arange(2 * KEEP_LAT, dtype=jnp.int32) - KEEP_LAT
    wavenumber = lax.axis_index("space") * share + jnp.arange(share, dtype=jnp.int32)
    weight = mode_mask(signed, wavenumber, kept_modes[0, 0], kept_modes[0, 1])
    grad_spec = grad_spec * weight
    spectrum = spectrum.reshape(nblocks, 2 * width, -1)
    grad_spec = grad_spec.reshape(nblocks, 2 * width, -1)
    grad_modes, grad_w_in, grad_b_in, grad_w_out, grad_b_out = backprop(
        spectrum, grad_spec, weight_in[0], bias_in[0], weight_out[0]
    )
    grad_modes = grad_modes.reshape(nblocks, 2, width, 2 * KEEP_LAT, share)
    rows = LAT // ndev
    back = lat_inverse_split(grad_modes, lat_cos, lat_sin, ndev).reshape(ndev, -1)
    parts = (grad_w_in, grad_b_in, grad_w_out, grad_b_out)
    flat = jnp.concatenate([p.reshape(-1) for p in parts])
    pad = (-flat.shape[0]) % ndev
    pieces = jnp.pad(flat, (0, pad)).reshape(ndev, -1)
    joined, received = lax.optimization_barrier((jnp.concatenate([back, pieces], axis=1), received))
    moved = lax.all_to_all(joined, "space", split_axis=0, concat_axis=0, tiled=True)
    rows_back = moved[:, : back.shape[1]].reshape(ndev, 2, nblocks, width, rows, share)
    mine = jnp.sum(moved[:, back.shape[1]:], axis=0)
    spread = jnp.broadcast_to(mine[None], pieces.shape)
    flat = lax.all_to_all(spread, "space", split_axis=0, concat_axis=0, tiled=True)
    flat = flat.reshape(-1)[: flat.size - pad]
    inverse = lon_inverse_split(rows_back, lon_cos, lon_sin, ndev)
    factor = 1.0 / math.sqrt(2 * KEEP_LAT * KEEP_LON)
    flat = flat * factor
    sums = []
    start = 0
    for p in parts:
        sums.append(flat[start:start + p.size].reshape(p.shape)[None])
        start += p.size
    upstream = jnp.where(section_index == last_section, own_grad, received)
    grad_field = (upstream.astype(jnp.float32) + inverse).astype(jnp.bfloat16)
    return (grad_field[None], *sums)


def solution(mesh):
    return jax.shard_map(
        shards,
        mesh=mesh,
        in_specs=(
            P("pipe", None, None, "space", None),
            P("pipe", None, None, "space", None),
            P("pipe", None),
            P("pipe", None, None, None, None),
            P("pipe", None, None, None),
            P("pipe", None, None, None, None),
        ),
        out_specs=(
            P("pipe", None, None, "space", None),
            P("pipe", None, None, None, None),
            P("pipe", None, None, None),
            P("pipe", None, None, None, None),
            P("pipe", None, None, None),
        ),
        check_vma=False,
    )
```

```python
import math

import jax
import numpy as np
import jax.numpy as jnp
from jax import lax
from jax.sharding import PartitionSpec as P

LAT = 256
LON = 512
KEEP_LON = 128
KEEP_LAT = 64


HIGHEST = lax.Precision.HIGH


def from_behind(block, axis, distance):
    devices = range(lax.axis_size(axis))
    route = [(i - distance, i) for i in devices if i - distance in devices]
    return lax.ppermute(block, axis, route)


def lon_tables(length, count):
    column = jnp.arange(length, dtype=jnp.int32)
    number = jnp.arange(count, dtype=jnp.int32)
    phase = column[:, None] * number[None, :] % length
    angle = phase.astype(jnp.float32) * (2.0 * math.pi / length)
    factor = 1.0 / math.sqrt(length)
    return (jnp.cos(angle) * factor, jnp.sin(angle) * factor)


def lat_tables(length, half):
    signed = jnp.arange(2 * half, dtype=jnp.int32) - half
    row_index = jnp.arange(length, dtype=jnp.int32)
    phase = signed[:, None] * row_index[None, :] % length
    angle = phase.astype(jnp.float32) * (2.0 * math.pi / length)
    factor = 1.0 / math.sqrt(length)
    return (jnp.cos(angle) * factor, jnp.sin(angle) * factor)


def lon_forward_constant(length, count, ndev):
    column = np.arange(length, dtype=np.int64)
    number = np.arange(count, dtype=np.int64)
    angle = (column[:, None] * number[None, :] % length).astype(np.float64) * (2.0 * math.pi / length)
    factor = 1.0 / math.sqrt(length)
    share = count // ndev
    cos_g = (np.cos(angle) * factor).reshape(length, ndev, 1, share)
    sin_g = -(np.sin(angle) * factor).reshape(length, ndev, 1, share)
    table = np.concatenate([cos_g, sin_g], axis=2).reshape(length, -1)
    return jnp.asarray(table.astype(np.float32))


def lon_forward_table(cos_table, sin_table, ndev):
    share = cos_table.shape[1] // ndev
    cos_g = cos_table.reshape(-1, ndev, 1, share)
    sin_g = -sin_table.reshape(-1, ndev, 1, share)
    return jnp.concatenate([cos_g, sin_g], axis=2).reshape(cos_table.shape[0], -1)


def lon_forward(field, table):
    values = field.astype(jnp.float32)
    return jnp.einsum("ibln,nc->iblc", values, table, precision=HIGHEST)


def lat_forward(spectrum, cos_table, sin_table):
    top = jnp.stack([cos_table, sin_table], axis=1)
    bottom = jnp.stack([-sin_table, cos_table], axis=1)
    table = jnp.stack([top, bottom])
    return jnp.einsum("ofpl,iblpj->iobfj", table, spectrum, precision=HIGHEST)


def lat_inverse(spectrum, cos_table, sin_table):
    top = jnp.stack([cos_table, -sin_table])
    bottom = jnp.stack([sin_table, cos_table])
    table = jnp.stack([top, bottom])
    return jnp.einsum("opfl,pibfj->oiblj", table, spectrum, precision=HIGHEST)


def lon_inverse(spectrum, cos_table, sin_table):
    table = jnp.stack([cos_table, -sin_table])
    return jnp.einsum("piblk,pnk->ibln", spectrum, table, precision=HIGHEST)


def lat_inverse_split(spectrum, cos_table, sin_table, ndev):
    top = jnp.stack([cos_table, -sin_table])
    bottom = jnp.stack([sin_table, cos_table])
    table = jnp.stack([top, bottom])
    table = table.reshape(table.shape[:3] + (ndev, -1))
    return jnp.einsum("opfdr,ipbfj->doibrj", table, spectrum, precision=HIGHEST)


def lon_inverse_split(spectrum, cos_table, sin_table, ndev):
    table = jnp.stack([cos_table, -sin_table])
    table = table.reshape(table.shape[:2] + (ndev, -1))
    return jnp.einsum("dpiblj,pndj->ibln", spectrum, table, precision=HIGHEST)


def mode_mask(signed, wavenumber, keep_lon, keep_lat):
    lat_kept = (signed >= -keep_lat) & (signed < keep_lat)
    lon_kept = wavenumber < keep_lon
    factor = jnp.where(wavenumber == 0, 1.0, 2.0).astype(jnp.float32)
    return (lat_kept[:, None] & lon_kept[None, :]).astype(jnp.float32) * factor[None, :]


def real_form(weights):
    real_part, imag_part = weights[0], weights[1]
    top = jnp.concatenate([real_part, -imag_part], axis=2)
    bottom = jnp.concatenate([imag_part, real_part], axis=2)
    return jnp.concatenate([top, bottom], axis=1)


def apply(weights, values):
    return jnp.einsum("kij,kjm->kim", weights, values, precision=HIGHEST)


def apply_adjoint(weights, values):
    return jnp.einsum("kji,kjm->kim", weights, values, precision=HIGHEST)


def complex_outer(left, right, width):
    full = jnp.einsum("kim,kjm->kij", left, right, precision=HIGHEST)
    full = full.reshape(full.shape[0], 2, width, 2, width)
    real_part = full[:, 0, :, 0] + full[:, 1, :, 1]
    imag_part = full[:, 1, :, 0] - full[:, 0, :, 1]
    return jnp.stack([real_part, imag_part])


def gelu_pair(values):
    inner = 0.7978845608 * (values + 0.044715 * values * values * values)
    tangent = jnp.tanh(inner)
    output = 0.5 * values * (1.0 + tangent)
    slope = 0.5 * (1.0 + tangent) + 0.5 * values * (1.0 - tangent * tangent) * 0.7978845608 * (
        1.0 + 3.0 * 0.044715 * values * values
    )
    return (output, slope)


def split_parts(stacked, width):
    return jnp.swapaxes(stacked.reshape(stacked.shape[0], 2, width), 0, 1)


def backprop(spectrum, grad_spec, weight_in, bias_in, weight_out):
    width = weight_in.shape[-1]
    forward_in = real_form(weight_in)
    forward_out = real_form(weight_out)
    bias = jnp.concatenate([bias_in[0], bias_in[1]], axis=1)
    before = apply(forward_in, spectrum) + bias[..., None]
    hidden, slope = gelu_pair(before)
    grad_hidden = apply_adjoint(forward_out, grad_spec)
    grad_before = grad_hidden * slope
    grad_modes = apply_adjoint(forward_in, grad_before)
    grad_w_out = complex_outer(grad_spec, hidden, width)
    grad_w_in = complex_outer(grad_before, spectrum, width)
    return (
        grad_modes,
        grad_w_in,
        split_parts(jnp.sum(grad_before, axis=-1), width),
        grad_w_out,
        split_parts(jnp.sum(grad_spec, axis=-1), width),
    )


def to_columns(spectrum, ndev):
    moved = lax.all_to_all(spectrum, "space", split_axis=3, concat_axis=2, tiled=True)
    nblocks, width, rows, _ = moved.shape
    return moved.reshape(nblocks, width, rows, 2, -1)


def sum_over(flat, axis):
    n = lax.axis_size(axis)
    pad = (-flat.shape[0]) % n
    pieces = jnp.pad(flat, (0, pad)).reshape(n, -1)
    got = lax.all_to_all(pieces, axis, split_axis=0, concat_axis=0, tiled=True)
    mine = jnp.sum(got, axis=0)
    spread = jnp.broadcast_to(mine[None], pieces.shape)
    full = lax.all_to_all(spread, axis, split_axis=0, concat_axis=0, tiled=True)
    return full.reshape(-1)[: flat.shape[0]]


def shards(activations, cotangent, kept_modes, weight_in, bias_in, weight_out):
    field = activations[0]
    own_grad = cotangent[0]
    nblocks = field.shape[0]
    width = field.shape[1]
    ndev = lax.axis_size("space")
    received = from_behind(own_grad, "pipe", -1)
    section_index = lax.axis_index("pipe")
    last_section = lax.axis_size("pipe") - 1
    lon_cos, lon_sin = lon_tables(LON, KEEP_LON)
    lat_cos, lat_sin = lat_tables(LAT, KEEP_LAT)
    table = lon_forward_constant(LON, KEEP_LON, ndev)
    col_field = to_columns(lon_forward(field, table), ndev)
    col_field, received = lax.optimization_barrier((col_field, received))
    spectrum = lat_forward(col_field, lat_cos, lat_sin)
    upstream = jnp.where(section_index == last_section, own_grad, received)
    col_grad = to_columns(lon_forward(upstream, table), ndev)
    grad_spec = lat_forward(col_grad, lat_cos, lat_sin)
    share = KEEP_LON // ndev
    signed = jnp.arange(2 * KEEP_LAT, dtype=jnp.int32) - KEEP_LAT
    wavenumber = lax.axis_index("space") * share + jnp.arange(share, dtype=jnp.int32)
    weight = mode_mask(signed, wavenumber, kept_modes[0, 0], kept_modes[0, 1])
    grad_spec = grad_spec * weight
    spectrum = spectrum.reshape(nblocks, 2 * width, -1)
    grad_spec = grad_spec.reshape(nblocks, 2 * width, -1)
    grad_modes, grad_w_in, grad_b_in, grad_w_out, grad_b_out = backprop(
        spectrum, grad_spec, weight_in[0], bias_in[0], weight_out[0]
    )
    grad_modes = grad_modes.reshape(nblocks, 2, width, 2 * KEEP_LAT, share)
    rows = LAT // ndev
    back = lat_inverse_split(grad_modes, lat_cos, lat_sin, ndev).reshape(ndev, -1)
    parts = (grad_w_in, grad_b_in, grad_w_out, grad_b_out)
    flat = jnp.concatenate([p.reshape(-1) for p in parts])
    pad = (-flat.shape[0]) % ndev
    pieces = jnp.pad(flat, (0, pad)).reshape(ndev, -1)
    moved = lax.all_to_all(
        jnp.concatenate([back, pieces], axis=1), "space", split_axis=0, concat_axis=0, tiled=True
    )
    rows_back = moved[:, : back.shape[1]].reshape(ndev, 2, nblocks, width, rows, share)
    mine = jnp.sum(moved[:, back.shape[1]:], axis=0)
    spread = jnp.broadcast_to(mine[None], pieces.shape)
    flat = lax.all_to_all(spread, "space", split_axis=0, concat_axis=0, tiled=True)
    flat = flat.reshape(-1)[: flat.size - pad]
    inverse = lon_inverse_split(rows_back, lon_cos, lon_sin, ndev)
    factor = 1.0 / math.sqrt(2 * KEEP_LAT * KEEP_LON)
    flat = flat * factor
    sums = []
    start = 0
    for p in parts:
        sums.append(flat[start:start + p.size].reshape(p.shape)[None])
        start += p.size
    grad_field = (upstream.astype(jnp.float32) + inverse).astype(jnp.bfloat16)
    return (grad_field[None], *sums)


def solution(mesh):
    return jax.shard_map(
        shards,
        mesh=mesh,
        in_specs=(
            P("pipe", None, None, "space", None),
            P("pipe", None, None, "space", None),
            P("pipe", None),
            P("pipe", None, None, None, None),
            P("pipe", None, None, None),
            P("pipe", None, None, None, None),
        ),
        out_specs=(
            P("pipe", None, None, "space", None),
            P("pipe", None, None, None, None),
            P("pipe", None, None, None),
            P("pipe", None, None, None, None),
            P("pipe", None, None, None),
        ),
        check_vma=False,
    )
```

```python
import math

import jax
import numpy as np
import jax.numpy as jnp
from jax import lax
from jax.sharding import PartitionSpec as P

LAT = 256
LON = 512
KEEP_LON = 128
KEEP_LAT = 64


HIGHEST = lax.Precision.HIGH


def from_behind(block, axis, distance):
    devices = range(lax.axis_size(axis))
    route = [(i - distance, i) for i in devices if i - distance in devices]
    return lax.ppermute(block, axis, route)


def lon_tables(length, count):
    column = jnp.arange(length, dtype=jnp.int32)
    number = jnp.arange(count, dtype=jnp.int32)
    phase = column[:, None] * number[None, :] % length
    angle = phase.astype(jnp.float32) * (2.0 * math.pi / length)
    factor = 1.0 / math.sqrt(length)
    return (jnp.cos(angle) * factor, jnp.sin(angle) * factor)


def lat_tables(length, half):
    signed = jnp.arange(2 * half, dtype=jnp.int32) - half
    row_index = jnp.arange(length, dtype=jnp.int32)
    phase = signed[:, None] * row_index[None, :] % length
    angle = phase.astype(jnp.float32) * (2.0 * math.pi / length)
    factor = 1.0 / math.sqrt(length)
    return (jnp.cos(angle) * factor, jnp.sin(angle) * factor)


def lon_forward_constant(length, count, ndev):
    column = np.arange(length, dtype=np.int64)
    number = np.arange(count, dtype=np.int64)
    angle = (column[:, None] * number[None, :] % length).astype(np.float64) * (2.0 * math.pi / length)
    factor = 1.0 / math.sqrt(length)
    share = count // ndev
    cos_g = (np.cos(angle) * factor).reshape(length, ndev, 1, share)
    sin_g = -(np.sin(angle) * factor).reshape(length, ndev, 1, share)
    table = np.concatenate([cos_g, sin_g], axis=2).reshape(length, -1)
    return jnp.asarray(table.astype(np.float32))


def lon_forward_table(cos_table, sin_table, ndev):
    share = cos_table.shape[1] // ndev
    cos_g = cos_table.reshape(-1, ndev, 1, share)
    sin_g = -sin_table.reshape(-1, ndev, 1, share)
    return jnp.concatenate([cos_g, sin_g], axis=2).reshape(cos_table.shape[0], -1)


def lon_forward(field, table):
    values = field.astype(jnp.float32)
    return jnp.einsum("ibln,nc->iblc", values, table, precision=HIGHEST)


def lat_forward(spectrum, cos_table, sin_table):
    top = jnp.stack([cos_table, sin_table], axis=1)
    bottom = jnp.stack([-sin_table, cos_table], axis=1)
    table = jnp.stack([top, bottom])
    return jnp.einsum("ofpl,iblpj->iobfj", table, spectrum, precision=HIGHEST)


def lat_inverse(spectrum, cos_table, sin_table):
    top = jnp.stack([cos_table, -sin_table])
    bottom = jnp.stack([sin_table, cos_table])
    table = jnp.stack([top, bottom])
    return jnp.einsum("opfl,pibfj->oiblj", table, spectrum, precision=HIGHEST)


def lon_inverse(spectrum, cos_table, sin_table):
    table = jnp.stack([cos_table, -sin_table])
    return jnp.einsum("piblk,pnk->ibln", spectrum, table, precision=HIGHEST)


def lat_inverse_split(spectrum, cos_table, sin_table, ndev):
    top = jnp.stack([cos_table, -sin_table])
    bottom = jnp.stack([sin_table, cos_table])
    table = jnp.stack([top, bottom])
    table = table.reshape(table.shape[:3] + (ndev, -1))
    return jnp.einsum("opfdr,ipbfj->doibrj", table, spectrum, precision=HIGHEST)


def lon_inverse_split(spectrum, cos_table, sin_table, ndev):
    table = jnp.stack([cos_table, -sin_table])
    table = table.reshape(table.shape[:2] + (ndev, -1))
    return jnp.einsum("dpiblj,pndj->ibln", spectrum, table, precision=HIGHEST)


def mode_mask(signed, wavenumber, keep_lon, keep_lat):
    lat_kept = (signed >= -keep_lat) & (signed < keep_lat)
    lon_kept = wavenumber < keep_lon
    factor = jnp.where(wavenumber == 0, 1.0, 2.0).astype(jnp.float32)
    return (lat_kept[:, None] & lon_kept[None, :]).astype(jnp.float32) * factor[None, :]


def real_form(weights):
    real_part, imag_part = weights[0], weights[1]
    top = jnp.concatenate([real_part, -imag_part], axis=2)
    bottom = jnp.concatenate([imag_part, real_part], axis=2)
    return jnp.concatenate([top, bottom], axis=1)


def apply(weights, values):
    return jnp.einsum("kij,kjm->kim", weights, values, precision=HIGHEST)


def apply_adjoint(weights, values):
    return jnp.einsum("kji,kjm->kim", weights, values, precision=HIGHEST)


def complex_outer(left, right, width):
    full = jnp.einsum("kim,kjm->kij", left, right, precision=HIGHEST)
    full = full.reshape(full.shape[0], 2, width, 2, width)
    real_part = full[:, 0, :, 0] + full[:, 1, :, 1]
    imag_part = full[:, 1, :, 0] - full[:, 0, :, 1]
    return jnp.stack([real_part, imag_part])


def gelu_pair(values):
    inner = 0.7978845608 * (values + 0.044715 * values * values * values)
    tangent = jnp.tanh(inner)
    output = 0.5 * values * (1.0 + tangent)
    slope = 0.5 * (1.0 + tangent) + 0.5 * values * (1.0 - tangent * tangent) * 0.7978845608 * (
        1.0 + 3.0 * 0.044715 * values * values
    )
    return (output, slope)


def split_parts(stacked, width):
    return jnp.swapaxes(stacked.reshape(stacked.shape[0], 2, width), 0, 1)


def backprop(spectrum, grad_spec, weight_in, bias_in, weight_out):
    width = weight_in.shape[-1]
    forward_in = real_form(weight_in)
    forward_out = real_form(weight_out)
    bias = jnp.concatenate([bias_in[0], bias_in[1]], axis=1)
    before = apply(forward_in, spectrum) + bias[..., None]
    hidden, slope = gelu_pair(before)
    grad_hidden = apply_adjoint(forward_out, grad_spec)
    grad_before = grad_hidden * slope
    grad_modes = apply_adjoint(forward_in, grad_before)
    grad_w_out = complex_outer(grad_spec, hidden, width)
    grad_w_in = complex_outer(grad_before, spectrum, width)
    return (
        grad_modes,
        grad_w_in,
        split_parts(jnp.sum(grad_before, axis=-1), width),
        grad_w_out,
        split_parts(jnp.sum(grad_spec, axis=-1), width),
    )


def to_columns(spectrum, ndev):
    moved = lax.all_to_all(spectrum, "space", split_axis=3, concat_axis=2, tiled=True)
    nblocks, width, rows, _ = moved.shape
    return moved.reshape(nblocks, width, rows, 2, -1)


def sum_over(flat, axis):
    n = lax.axis_size(axis)
    pad = (-flat.shape[0]) % n
    pieces = jnp.pad(flat, (0, pad)).reshape(n, -1)
    got = lax.all_to_all(pieces, axis, split_axis=0, concat_axis=0, tiled=True)
    mine = jnp.sum(got, axis=0)
    spread = jnp.broadcast_to(mine[None], pieces.shape)
    full = lax.all_to_all(spread, axis, split_axis=0, concat_axis=0, tiled=True)
    return full.reshape(-1)[: flat.shape[0]]


def shards(activations, cotangent, kept_modes, weight_in, bias_in, weight_out):
    field = activations[0]
    own_grad = cotangent[0]
    nblocks = field.shape[0]
    width = field.shape[1]
    ndev = lax.axis_size("space")
    received = from_behind(own_grad, "pipe", -1)
    section_index = lax.axis_index("pipe")
    last_section = lax.axis_size("pipe") - 1
    lon_cos, lon_sin = lon_tables(LON, KEEP_LON)
    lat_cos, lat_sin = lat_tables(LAT, KEEP_LAT)
    table = lon_forward_constant(LON, KEEP_LON, ndev)
    col_field = to_columns(lon_forward(field, table), ndev)
    upstream = jnp.where(section_index == last_section, own_grad, received)
    col_field, lon_grad = lax.optimization_barrier((col_field, lon_forward(upstream, table)))
    spectrum = lat_forward(col_field, lat_cos, lat_sin)
    col_grad = to_columns(lon_grad, ndev)
    grad_spec = lat_forward(col_grad, lat_cos, lat_sin)
    share = KEEP_LON // ndev
    signed = jnp.arange(2 * KEEP_LAT, dtype=jnp.int32) - KEEP_LAT
    wavenumber = lax.axis_index("space") * share + jnp.arange(share, dtype=jnp.int32)
    weight = mode_mask(signed, wavenumber, kept_modes[0, 0], kept_modes[0, 1])
    grad_spec = grad_spec * weight
    spectrum = spectrum.reshape(nblocks, 2 * width, -1)
    grad_spec = grad_spec.reshape(nblocks, 2 * width, -1)
    grad_modes, grad_w_in, grad_b_in, grad_w_out, grad_b_out = backprop(
        spectrum, grad_spec, weight_in[0], bias_in[0], weight_out[0]
    )
    grad_modes = grad_modes.reshape(nblocks, 2, width, 2 * KEEP_LAT, share)
    rows = LAT // ndev
    back = lat_inverse_split(grad_modes, lat_cos, lat_sin, ndev).reshape(ndev, -1)
    parts = (grad_w_in, grad_b_in, grad_w_out, grad_b_out)
    flat = jnp.concatenate([p.reshape(-1) for p in parts])
    pad = (-flat.shape[0]) % ndev
    pieces = jnp.pad(flat, (0, pad)).reshape(ndev, -1)
    moved = lax.all_to_all(
        jnp.concatenate([back, pieces], axis=1), "space", split_axis=0, concat_axis=0, tiled=True
    )
    rows_back = moved[:, : back.shape[1]].reshape(ndev, 2, nblocks, width, rows, share)
    mine = jnp.sum(moved[:, back.shape[1]:], axis=0)
    spread = jnp.broadcast_to(mine[None], pieces.shape)
    flat = lax.all_to_all(spread, "space", split_axis=0, concat_axis=0, tiled=True)
    flat = flat.reshape(-1)[: flat.size - pad]
    inverse = lon_inverse_split(rows_back, lon_cos, lon_sin, ndev)
    factor = 1.0 / math.sqrt(2 * KEEP_LAT * KEEP_LON)
    flat = flat * factor
    sums = []
    start = 0
    for p in parts:
        sums.append(flat[start:start + p.size].reshape(p.shape)[None])
        start += p.size
    grad_field = (upstream.astype(jnp.float32) + inverse).astype(jnp.bfloat16)
    return (grad_field[None], *sums)


def solution(mesh):
    return jax.shard_map(
        shards,
        mesh=mesh,
        in_specs=(
            P("pipe", None, None, "space", None),
            P("pipe", None, None, "space", None),
            P("pipe", None),
            P("pipe", None, None, None, None),
            P("pipe", None, None, None),
            P("pipe", None, None, None, None),
        ),
        out_specs=(
            P("pipe", None, None, "space", None),
            P("pipe", None, None, None, None),
            P("pipe", None, None, None),
            P("pipe", None, None, None, None),
            P("pipe", None, None, None),
        ),
        check_vma=False,
    )
```

```python
import math

import jax
import numpy as np
import jax.numpy as jnp
from jax import lax
from jax.sharding import PartitionSpec as P

LAT = 256
LON = 512
KEEP_LON = 128
KEEP_LAT = 64


HIGHEST = lax.Precision.HIGH


def from_behind(block, axis, distance):
    devices = range(lax.axis_size(axis))
    route = [(i - distance, i) for i in devices if i - distance in devices]
    return lax.ppermute(block, axis, route)


def lon_tables(length, count):
    column = jnp.arange(length, dtype=jnp.int32)
    number = jnp.arange(count, dtype=jnp.int32)
    phase = column[:, None] * number[None, :] % length
    angle = phase.astype(jnp.float32) * (2.0 * math.pi / length)
    factor = 1.0 / math.sqrt(length)
    return (jnp.cos(angle) * factor, jnp.sin(angle) * factor)


def lat_tables(length, half):
    signed = jnp.arange(2 * half, dtype=jnp.int32) - half
    row_index = jnp.arange(length, dtype=jnp.int32)
    phase = signed[:, None] * row_index[None, :] % length
    angle = phase.astype(jnp.float32) * (2.0 * math.pi / length)
    factor = 1.0 / math.sqrt(length)
    return (jnp.cos(angle) * factor, jnp.sin(angle) * factor)


def lon_forward_constant(length, count, ndev):
    column = np.arange(length, dtype=np.int64)
    number = np.arange(count, dtype=np.int64)
    angle = (column[:, None] * number[None, :] % length).astype(np.float64) * (2.0 * math.pi / length)
    factor = 1.0 / math.sqrt(length)
    share = count // ndev
    cos_g = (np.cos(angle) * factor).reshape(length, ndev, 1, share)
    sin_g = -(np.sin(angle) * factor).reshape(length, ndev, 1, share)
    table = np.concatenate([cos_g, sin_g], axis=2).reshape(length, -1)
    return jnp.asarray(table.astype(np.float32))


def lon_forward_table(cos_table, sin_table, ndev):
    share = cos_table.shape[1] // ndev
    cos_g = cos_table.reshape(-1, ndev, 1, share)
    sin_g = -sin_table.reshape(-1, ndev, 1, share)
    return jnp.concatenate([cos_g, sin_g], axis=2).reshape(cos_table.shape[0], -1)


def lon_forward(field, table):
    values = field.astype(jnp.float32)
    return jnp.einsum("ibln,nc->iblc", values, table, precision=HIGHEST)


def lat_forward(spectrum, cos_table, sin_table):
    top = jnp.stack([cos_table, sin_table], axis=1)
    bottom = jnp.stack([-sin_table, cos_table], axis=1)
    table = jnp.stack([top, bottom])
    return jnp.einsum("ofpl,iblpj->iobfj", table, spectrum, precision=HIGHEST)


def lat_inverse(spectrum, cos_table, sin_table):
    top = jnp.stack([cos_table, -sin_table])
    bottom = jnp.stack([sin_table, cos_table])
    table = jnp.stack([top, bottom])
    return jnp.einsum("opfl,pibfj->oiblj", table, spectrum, precision=HIGHEST)


def lon_inverse(spectrum, cos_table, sin_table):
    table = jnp.stack([cos_table, -sin_table])
    return jnp.einsum("piblk,pnk->ibln", spectrum, table, precision=HIGHEST)


def lat_inverse_split(spectrum, cos_table, sin_table, ndev):
    top = jnp.stack([cos_table, -sin_table])
    bottom = jnp.stack([sin_table, cos_table])
    table = jnp.stack([top, bottom])
    table = table.reshape(table.shape[:3] + (ndev, -1))
    return jnp.einsum("opfdr,ipbfj->doibrj", table, spectrum, precision=HIGHEST)


def lon_inverse_split(spectrum, cos_table, sin_table, ndev):
    table = jnp.stack([cos_table, -sin_table])
    table = table.reshape(table.shape[:2] + (ndev, -1))
    return jnp.einsum("dpiblj,pndj->ibln", spectrum, table, precision=HIGHEST)


def mode_mask(signed, wavenumber, keep_lon, keep_lat):
    lat_kept = (signed >= -keep_lat) & (signed < keep_lat)
    lon_kept = wavenumber < keep_lon
    factor = jnp.where(wavenumber == 0, 1.0, 2.0).astype(jnp.float32)
    return (lat_kept[:, None] & lon_kept[None, :]).astype(jnp.float32) * factor[None, :]


def real_form(weights):
    real_part, imag_part = weights[0], weights[1]
    top = jnp.concatenate([real_part, -imag_part], axis=2)
    bottom = jnp.concatenate([imag_part, real_part], axis=2)
    return jnp.concatenate([top, bottom], axis=1)


def apply(weights, values):
    return jnp.einsum("kij,kjm->kim", weights, values, precision=HIGHEST)


def apply_adjoint(weights, values):
    return jnp.einsum("kji,kjm->kim", weights, values, precision=HIGHEST)


def complex_outer(left, right, width):
    full = jnp.einsum("kim,kjm->kij", left, right, precision=HIGHEST)
    full = full.reshape(full.shape[0], 2, width, 2, width)
    real_part = full[:, 0, :, 0] + full[:, 1, :, 1]
    imag_part = full[:, 1, :, 0] - full[:, 0, :, 1]
    return jnp.stack([real_part, imag_part])


def gelu_pair(values):
    inner = 0.7978845608 * (values + 0.044715 * values * values * values)
    tangent = jnp.tanh(inner)
    output = 0.5 * values * (1.0 + tangent)
    slope = 0.5 * (1.0 + tangent) + 0.5 * values * (1.0 - tangent * tangent) * 0.7978845608 * (
        1.0 + 3.0 * 0.044715 * values * values
    )
    return (output, slope)


def split_parts(stacked, width):
    return jnp.swapaxes(stacked.reshape(stacked.shape[0], 2, width), 0, 1)


def backprop(spectrum, grad_spec, weight_in, bias_in, weight_out):
    width = weight_in.shape[-1]
    forward_in = real_form(weight_in)
    forward_out = real_form(weight_out)
    bias = jnp.concatenate([bias_in[0], bias_in[1]], axis=1)
    before = apply(forward_in, spectrum) + bias[..., None]
    hidden, slope = gelu_pair(before)
    grad_hidden = apply_adjoint(forward_out, grad_spec)
    grad_before = grad_hidden * slope
    grad_modes = apply_adjoint(forward_in, grad_before)
    grad_w_out = complex_outer(grad_spec, hidden, width)
    grad_w_in = complex_outer(grad_before, spectrum, width)
    return (
        grad_modes,
        grad_w_in,
        split_parts(jnp.sum(grad_before, axis=-1), width),
        grad_w_out,
        split_parts(jnp.sum(grad_spec, axis=-1), width),
    )


def to_columns(spectrum, ndev):
    moved = lax.all_to_all(spectrum, "space", split_axis=3, concat_axis=2, tiled=True)
    nblocks, width, rows, _ = moved.shape
    return moved.reshape(nblocks, width, rows, 2, -1)


def sum_over(flat, axis):
    n = lax.axis_size(axis)
    pad = (-flat.shape[0]) % n
    pieces = jnp.pad(flat, (0, pad)).reshape(n, -1)
    got = lax.all_to_all(pieces, axis, split_axis=0, concat_axis=0, tiled=True)
    mine = jnp.sum(got, axis=0)
    spread = jnp.broadcast_to(mine[None], pieces.shape)
    full = lax.all_to_all(spread, axis, split_axis=0, concat_axis=0, tiled=True)
    return full.reshape(-1)[: flat.shape[0]]


def shards(activations, cotangent, kept_modes, weight_in, bias_in, weight_out):
    field = activations[0]
    own_grad = cotangent[0]
    nblocks = field.shape[0]
    width = field.shape[1]
    ndev = lax.axis_size("space")
    section_index = lax.axis_index("pipe")
    last_section = lax.axis_size("pipe") - 1
    lon_cos, lon_sin = lon_tables(LON, KEEP_LON)
    lat_cos, lat_sin = lat_tables(LAT, KEEP_LAT)
    table = lon_forward_constant(LON, KEEP_LON, ndev)
    field_lon, own_grad = lax.optimization_barrier((lon_forward(field, table), own_grad))
    received = from_behind(own_grad, "pipe", -1)
    col_field = to_columns(field_lon, ndev)
    upstream = jnp.where(section_index == last_section, own_grad, received)
    col_field, lon_grad = lax.optimization_barrier((col_field, lon_forward(upstream, table)))
    spectrum = lat_forward(col_field, lat_cos, lat_sin)
    col_grad = to_columns(lon_grad, ndev)
    grad_spec = lat_forward(col_grad, lat_cos, lat_sin)
    share = KEEP_LON // ndev
    signed = jnp.arange(2 * KEEP_LAT, dtype=jnp.int32) - KEEP_LAT
    wavenumber = lax.axis_index("space") * share + jnp.arange(share, dtype=jnp.int32)
    weight = mode_mask(signed, wavenumber, kept_modes[0, 0], kept_modes[0, 1])
    grad_spec = grad_spec * weight
    spectrum = spectrum.reshape(nblocks, 2 * width, -1)
    grad_spec = grad_spec.reshape(nblocks, 2 * width, -1)
    grad_modes, grad_w_in, grad_b_in, grad_w_out, grad_b_out = backprop(
        spectrum, grad_spec, weight_in[0], bias_in[0], weight_out[0]
    )
    grad_modes = grad_modes.reshape(nblocks, 2, width, 2 * KEEP_LAT, share)
    rows = LAT // ndev
    back = lat_inverse_split(grad_modes, lat_cos, lat_sin, ndev).reshape(ndev, -1)
    parts = (grad_w_in, grad_b_in, grad_w_out, grad_b_out)
    flat = jnp.concatenate([p.reshape(-1) for p in parts])
    pad = (-flat.shape[0]) % ndev
    pieces = jnp.pad(flat, (0, pad)).reshape(ndev, -1)
    moved = lax.all_to_all(
        jnp.concatenate([back, pieces], axis=1), "space", split_axis=0, concat_axis=0, tiled=True
    )
    rows_back = moved[:, : back.shape[1]].reshape(ndev, 2, nblocks, width, rows, share)
    mine = jnp.sum(moved[:, back.shape[1]:], axis=0)
    spread = jnp.broadcast_to(mine[None], pieces.shape)
    flat = lax.all_to_all(spread, "space", split_axis=0, concat_axis=0, tiled=True)
    flat = flat.reshape(-1)[: flat.size - pad]
    inverse = lon_inverse_split(rows_back, lon_cos, lon_sin, ndev)
    factor = 1.0 / math.sqrt(2 * KEEP_LAT * KEEP_LON)
    flat = flat * factor
    sums = []
    start = 0
    for p in parts:
        sums.append(flat[start:start + p.size].reshape(p.shape)[None])
        start += p.size
    grad_field = (upstream.astype(jnp.float32) + inverse).astype(jnp.bfloat16)
    return (grad_field[None], *sums)


def solution(mesh):
    return jax.shard_map(
        shards,
        mesh=mesh,
        in_specs=(
            P("pipe", None, None, "space", None),
            P("pipe", None, None, "space", None),
            P("pipe", None),
            P("pipe", None, None, None, None),
            P("pipe", None, None, None),
            P("pipe", None, None, None, None),
        ),
        out_specs=(
            P("pipe", None, None, "space", None),
            P("pipe", None, None, None, None),
            P("pipe", None, None, None),
            P("pipe", None, None, None, None),
            P("pipe", None, None, None),
        ),
        check_vma=False,
    )
```
